256 devices in a mesh: dp: 64 (over z, y, core), mp: 4 (over x).
Axes of the slice: x: 4, y: 4, z: 8, core: 2. Of those that a mesh axis runs over, the one named last changes fastest.
Arguments:
- tree_query: bfloat16 [8192, 2048], P('dp', 'mp'), may hold values from -6 to 6
- new_kv: bfloat16 [8192, 2, 512], P('dp', None, 'mp'), may hold values from -6 to 6
- kv_cache: bfloat16 [2560, 2, 128, 512], P('dp', None, None, 'mp'), may hold values from -4 to 4
- page_table: int32 [128, 32], P('dp'), may hold values from 0 to 39, as said below
- cache_len: int32 [128], P('dp'), may hold values from 2 to 4096, as said below
- tree_mask: int32 [128, 64, 64], P('dp'), may hold values from 0 to 1, as said below
- out_weight: bfloat16 [2048, 2048], P('mp'), may hold values from -0.5 to 0.5
- residual_in: bfloat16 [8192, 2048], P('dp'), may hold values from -3 to 3
- norm_gain: float32 [2048], replicated, may hold values from 0.25 to 1.75
- route_ids: int32 [8192, 6], P('dp'), may hold values from 0 to 63, all different within a row; in each aligned block of 128 rows (0 to 127, 128 to 255, ...) at most 16 rows name the same one
- route_weight: float32 [8192, 6], P('dp'), may hold values from 0.05 to 0.5
- w_gate: bfloat16 [64, 2048, 1408], P('dp', None, 'mp'), may hold values from -0.125 to 0.125
- w_up: bfloat16 [64, 2048, 1408], P('dp', None, 'mp'), may hold values from -0.125 to 0.125
- w_down: bfloat16 [64, 1408, 2048], P('dp', None, 'mp'), may hold values from -0.15625 to 0.15625
- shared_gate: bfloat16 [2048, 2816], P('dp', 'mp'), may hold values from -0.125 to 0.125
- shared_up: bfloat16 [2048, 2816], P('dp', 'mp'), may hold values from -0.125 to 0.125
- shared_down: bfloat16 [2816, 2048], P('mp', 'dp'), may hold values from -0.109375 to 0.109375
Outputs:
- layer_out: bfloat16 [8192, 2048], P('dp', 'mp')
The draws below stay inside these ranges and needn't reach their ends.
Inputs may be any that keep to these rules, and one draw needn't show every extreme that they name: `route_ids`: each row names 6 different experts. Within the rows of one index of dp (aligned blocks of 128 rows) no expert is named by more than 16 rows, and in some block one expert is named by exactly 16 rows. `cache_len`: the pages of the requests of one index of dp number at most 40 together; some request has exactly 4096 cached positions. `page_table`: entry [r, j] is the slot, in the pool of the index of dp that holds request r, of the page with cache positions j * 128 to j * 128 + 127. Entries with j * 128 < cache_len[r] are distinct over the requests of one index of dp; the other entries are valid slots whose contents are not read. tree_mask[r, i, u] is 1 where tree node u is node i or an ancestor of it, else 0; node 0 is the root and each other node's parent has a smaller index.
All inputs are finite; a program needn't handle non-finite values.
Results may differ from the reference program's by a relative error of at most 0.009.
Values may be sent and summed in bfloat16 or wider, within the bound.
No kernel may reach another device: no remote copies, remote signals or barrier semaphores. Data moves between devices by JAX's collectives and lax.ppermute only.
A program may use at most 128 MiB of HBM per device.

```python
import math
import jax
import jax.numpy as jnp
import numpy as np
from jax import lax

D = 2048
HEADS = 16
KV_HEADS = 4
HEAD_DIM = 128
FF = 1408
SHARED_FF = 2816
TOPK = 6
PAGE = 128
TREE = 64
MAXPAGES = 32
REQ_DEV = 2
EXPERTS = 64
TOK_DEV = 128
REQUESTS = 128
TOKENS = 8192
PAGES_DEV = 40
CACHE_PAGES = 2560
CAP = 16
N_DP = 64


def cache_plan(key):
    groups = REQUESTS // REQ_DEV
    subkeys = jax.random.split(jax.random.fold_in(key, 101), 6)
    levels = int(math.log2(MAXPAGES))
    long_pick = jax.random.randint(subkeys[0], (groups,), 0, REQ_DEV)
    exponents = jax.random.randint(subkeys[1], (groups,), 0, levels + 1)
    long_pages = jnp.left_shift(jnp.ones((groups,), jnp.int32), exponents)
    short_pages = jax.random.randint(subkeys[2], (groups, REQ_DEV), 1, 5)
    is_long = jnp.arange(REQ_DEV)[None, :] == long_pick[:, None]
    page_counts = jnp.where(is_long, long_pages[:, None], short_pages)
    tail_rows = jax.random.randint(subkeys[3], (groups, REQ_DEV), 2, PAGE + 1)
    forced = jax.random.randint(subkeys[4], (), 0, groups)
    full_group = (jnp.arange(groups)[:, None] == forced) & is_long
    page_counts = jnp.where(full_group, MAXPAGES, page_counts)
    tail_rows = jnp.where(full_group, PAGE, tail_rows)
    lengths = (page_counts - 1) * PAGE + tail_rows
    orders = jax.vmap(lambda subkey: jax.random.permutation(subkey, PAGES_DEV))(jax.random.split(subkeys[5], groups))
    offsets = jnp.cumsum(page_counts, axis=1) - page_counts
    columns = (offsets[:, :, None] + jnp.arange(MAXPAGES)[None, None, :]) % PAGES_DEV
    slot_table = jax.vmap(lambda order_row, column_rows: order_row[column_rows])(orders, columns)
    return (lengths.reshape(REQUESTS).astype(jnp.int32), slot_table.reshape(REQUESTS, MAXPAGES).astype(jnp.int32))


def draw_cache_len(key, part):
    return cache_plan(key)[0]


def draw_page_table(key, part):
    return cache_plan(key)[1]


def draw_tree_mask(key, part):
    limits = jnp.maximum(jnp.arange(TREE), 1)
    parents = jax.random.randint(jax.random.fold_in(key, 303), (REQUESTS, TREE), 0, limits[None, :])
    identity_rows = jnp.eye(TREE, dtype=jnp.int32)

    def add_node(node, ancestors):
        parent_rows = jax.vmap(lambda table_rows, parent: table_rows[parent])(ancestors, parents[:, node])
        parent_rows = jnp.where(node > 0, parent_rows, 0)
        new_row = jnp.maximum(parent_rows, identity_rows[node][None, :])
        return ancestors.at[:, node, :].set(new_row)
    ancestors = lax.fori_loop(0, TREE, add_node, jnp.zeros((REQUESTS, TREE, TREE), jnp.int32))
    return ancestors.astype(jnp.int32)


def draw_tree_query(key, part):
    shape = (TOKENS, HEADS * HEAD_DIM)
    values = jnp.clip(1.5 * jax.random.normal(jax.random.fold_in(key, 11), shape), -6.0, 6.0)
    return values.astype(jnp.bfloat16)


def draw_new_kv(key, part):
    shape = (TOKENS, 2, KV_HEADS * HEAD_DIM)
    values = jnp.clip(jax.random.normal(jax.random.fold_in(key, 13), shape), -4.0, 4.0)
    return values.astype(jnp.bfloat16)


def level_of(key, shape, cuts, low, high):
    loudness, own = 1.0, jax.random.fold_in(key, 6)
    for dim, parts in cuts:
        draws = jnp.exp(jax.random.uniform(jax.random.fold_in(own, dim), (parts,), jnp.float32, low / len(cuts), high / len(cuts)))
        loudness = loudness * jnp.repeat(draws, shape[dim] // parts).reshape([-1 if axis == dim else 1 for axis in range(len(shape))])
    return loudness


def deal_out(stream_key, own, number, rows, number_of, top, bound, lean):
    sequence = jax.random.permutation(stream_key, number_of)
    packed, ordinary = shares(number_of, rows * top, bound, lean, True), shares(number_of, rows * top, bound, lean, False)
    places = jnp.arange(number_of)

    def named(tallies, turn):
        used = int((tallies > 0).sum())
        fixed = max(1, used // 4)
        moved = fixed + (places - fixed + turn * (used - fixed)) % max(1, number_of - fixed)
        return jnp.zeros((number_of,), jnp.int32).at[sequence[jnp.where(places < fixed, places, moved)]].set(jnp.asarray(tallies, jnp.int32))

    tallies = jnp.where(number % 4 == 0, named(packed, number // 4), named(ordinary, number - number // 4 - 1))
    mixed = jax.random.permutation(jax.random.fold_in(own, 3), number_of)
    donor, taker = mixed[0:number_of // 2 * 2:2], mixed[1:number_of // 2 * 2:2]
    slack = jnp.minimum(tallies[donor] - 1, bound - tallies[taker]) // 2
    slack = jnp.where((donor == sequence[0]) | (taker == sequence[0]) | (tallies[taker] == 0), 0, jnp.maximum(slack, 0))
    moved = jax.random.randint(jax.random.fold_in(own, 4), (number_of // 2,), 0, 1 << 20) % (slack + 1)
    tallies = tallies.at[donor].add(-moved).at[taker].add(moved)
    items = jnp.searchsorted(jnp.cumsum(tallies), jnp.arange(rows * top), side="right").astype(jnp.int32)
    listing = items.reshape(top, rows).T
    listing = listing[jax.random.permutation(jax.random.fold_in(own, 1), rows)]
    turn = jax.random.randint(jax.random.fold_in(own, 2), (rows, 1), 0, top)
    return jnp.take_along_axis(listing, (jnp.arange(top)[None, :] + turn) % top, axis=1)


def shares(count, total, reach, lean, full):
    loads = [(1 << 20) // math.isqrt(grade ** lean) + 1 for grade in range(1, count + 1)]
    largest = reach if full else min(reach, max(-(-total // count), total * loads[0] // sum(loads)))
    least = 1 if total - largest >= count - 1 else 0
    given, surplus = [largest] + [least] * (count - 1), total - largest - least * (count - 1)
    while surplus > 0:
        movable = [i for i in range(1, count) if given[i] < largest] or [i for i in range(1, count) if given[i] < reach]
        pool, left = sum([loads[i] for i in movable]), surplus
        for i in movable:
            extra = min(reach - given[i], max(1, left * loads[i] // pool), surplus)
            given[i] = given[i] + extra
            surplus = surplus - extra
    return np.array(given)


def normal_values(stream_key, extent, spread, reach, cuts=(), kind=jnp.bfloat16):
    drawn = spread * jax.random.normal(stream_key, extent, jnp.float32)
    if cuts:
        drawn = drawn * level_of(stream_key, extent, cuts, -0.22, 0.18)
    return jnp.clip(drawn, -reach, reach).astype(kind)


def setup_inputs(seed: int = 0) -> dict:
    keys = jax.random.split(jax.random.key(seed), 18)
    tree_query = draw_tree_query(jax.random.fold_in(keys[17], 71), 0)
    new_kv = draw_new_kv(jax.random.fold_in(keys[17], 71), 0)
    kv_cache = normal_values(keys[2], (CACHE_PAGES, 2, PAGE, KV_HEADS * HEAD_DIM), 1.0, 4.0, ((0, 64), (3, 4)))
    page_table = draw_page_table(jax.random.fold_in(keys[17], 71), 0)
    cache_len = draw_cache_len(jax.random.fold_in(keys[17], 71), 0)
    tree_mask = draw_tree_mask(jax.random.fold_in(keys[17], 71), 0)
    out_weight = normal_values(keys[6], (HEADS * HEAD_DIM, D), (HEADS * HEAD_DIM // 16) ** -0.5, 0.5, ((0, 4),))
    residual_in = normal_values(keys[7], (TOKENS, D), 0.5, 3.0, ((0, 64),))
    norm_gain = jnp.clip(1.0 + 0.15 * jax.random.normal(keys[8], (D,), jnp.float32), 0.25, 1.75)
    route_ids_keys = jax.random.split(jax.random.fold_in(keys[9], 1), TOKENS // TOK_DEV)
    route_ids_turns = jax.random.permutation(jax.random.fold_in(keys[9], 3), TOKENS // TOK_DEV)
    route_ids = jax.vmap(lambda own, number: deal_out(jax.random.fold_in(keys[9], 2), own, number, TOK_DEV, EXPERTS, TOPK, CAP, 2))(route_ids_keys, route_ids_turns).reshape((TOKENS, TOPK))
    route_weight = jnp.clip(jnp.exp(math.log(0.5) - 2.3025851 * jax.random.uniform(keys[10], (TOKENS, TOPK), jnp.float32) ** level_of(keys[10], (TOKENS, TOPK), ((0, 64),), -0.2, 0.2)), 0.05, 0.5)
    w_gate = normal_values(keys[11], (EXPERTS, D, FF), D ** -0.5, 0.125, ((0, 64), (2, 4)))
    w_up = normal_values(keys[12], (EXPERTS, D, FF), D ** -0.5, 0.125, ((0, 64), (2, 4)))
    w_down = normal_values(keys[13], (EXPERTS, FF, D), FF ** -0.5, 0.15625, ((0, 64), (2, 4)))
    shared_gate = normal_values(keys[14], (D, SHARED_FF), D ** -0.5, 0.125, ((0, 64), (1, 4)))
    shared_up = normal_values(keys[15], (D, SHARED_FF), D ** -0.5, 0.125, ((0, 64), (1, 4)))
    shared_down = normal_values(keys[16], (SHARED_FF, D), SHARED_FF ** -0.5, 0.109375, ((0, 4), (1, 64)))
    return dict(tree_query=tree_query, new_kv=new_kv, kv_cache=kv_cache, page_table=page_table, cache_len=cache_len, tree_mask=tree_mask, out_weight=out_weight, residual_in=residual_in, norm_gain=norm_gain, route_ids=route_ids, route_weight=route_weight, w_gate=w_gate, w_up=w_up, w_down=w_down, shared_gate=shared_gate, shared_up=shared_up, shared_down=shared_down)


NEGATIVE_FILL = -1e+30
EPSILON = 1e-05

def normalize(rows, gain):
    values = rows.astype(jnp.float32)
    mean_square = lax.optimization_barrier(jnp.mean(values * values, axis=-1, keepdims=True))
    return (values * lax.rsqrt(mean_square + EPSILON) * gain).astype(jnp.bfloat16)

def reference(tree_query, new_kv, kv_cache, page_table, cache_len, tree_mask, out_weight, residual_in, norm_gain, route_ids, route_weight, w_gate, w_up, w_down, shared_gate, shared_up, shared_down):
    group_size = HEADS // KV_HEADS
    score_scale = HEAD_DIM ** (-0.5)

    def per_request(request):
        pool_base = request // REQ_DEV * PAGES_DEV
        kv_pages = kv_cache[pool_base + page_table[request]]
        cache_keys = kv_pages[:, 0].reshape(MAXPAGES * PAGE, KV_HEADS, HEAD_DIM).astype(jnp.float32)
        cache_values = kv_pages[:, 1].reshape(MAXPAGES * PAGE, KV_HEADS, HEAD_DIM).astype(jnp.float32)
        q_rows = lax.dynamic_slice_in_dim(tree_query, request * TREE, TREE, 0)
        q_rows = q_rows.reshape(TREE, KV_HEADS, group_size, HEAD_DIM).astype(jnp.float32)
        fresh_rows = lax.dynamic_slice_in_dim(new_kv, request * TREE, TREE, 0).astype(jnp.float32)
        tree_keys = fresh_rows[:, 0].reshape(TREE, KV_HEADS, HEAD_DIM)
        tree_values = fresh_rows[:, 1].reshape(TREE, KV_HEADS, HEAD_DIM)
        live_mask = jnp.arange(MAXPAGES * PAGE, dtype=jnp.int32) < cache_len[request]
        cache_scores = jnp.einsum('tgjd,kgd->gjtk', q_rows, cache_keys) * score_scale
        cache_scores = jnp.where(live_mask, cache_scores, NEGATIVE_FILL)
        tree_allow = tree_mask[request] == 1
        tree_scores = jnp.einsum('tgjd,ugd->gjtu', q_rows, tree_keys) * score_scale
        tree_scores = jnp.where(tree_allow, tree_scores, NEGATIVE_FILL)
        row_peak = jnp.maximum(lax.optimization_barrier(jnp.max(cache_scores, axis=-1)), lax.optimization_barrier(jnp.max(tree_scores, axis=-1)))[..., None]
        cache_probs = jnp.where(live_mask, jnp.exp(cache_scores - row_peak), 0.0)
        tree_probs = jnp.where(tree_allow, jnp.exp(tree_scores - row_peak), 0.0)
        denom_sum = lax.optimization_barrier(jnp.sum(cache_probs, axis=-1)) + lax.optimization_barrier(jnp.sum(tree_probs, axis=-1))
        cache_weights = lax.optimization_barrier(cache_probs.astype(jnp.bfloat16)).astype(jnp.float32)
        tree_weights = lax.optimization_barrier(tree_probs.astype(jnp.bfloat16)).astype(jnp.float32)
        weighted = jnp.einsum('gjtk,kgd->tgjd', cache_weights, cache_values)
        weighted = weighted + jnp.einsum('gjtu,ugd->tgjd', tree_weights, tree_values)
        result = weighted / jnp.transpose(denom_sum, (2, 0, 1))[..., None]
        return result.reshape(TREE, HEADS * HEAD_DIM).astype(jnp.bfloat16)
    attended = lax.map(per_request, jnp.arange(REQUESTS, dtype=jnp.int32)).reshape(TOKENS, HEADS * HEAD_DIM)
    projected = jnp.dot(attended, out_weight, preferred_element_type=jnp.float32)
    stream = (residual_in.astype(jnp.float32) + projected).astype(jnp.bfloat16)
    normed = normalize(stream, norm_gain)
    shared_gate_proj = jnp.dot(normed, shared_gate, preferred_element_type=jnp.float32)
    shared_up_proj = jnp.dot(normed, shared_up, preferred_element_type=jnp.float32)
    shared_hidden = (jax.nn.silu(shared_gate_proj) * shared_up_proj).astype(jnp.bfloat16)
    shared_out = jnp.dot(shared_hidden, shared_down, preferred_element_type=jnp.float32).astype(jnp.bfloat16)
    shared_out = lax.optimization_barrier(shared_out).astype(jnp.float32)
    block_ids = route_ids.reshape(N_DP, TOK_DEV * TOPK)
    onehot = (block_ids[..., None] == jnp.arange(EXPERTS, dtype=jnp.int32)).astype(jnp.int32)
    slot_index = lax.optimization_barrier(jnp.sum((jnp.cumsum(onehot, axis=1) - onehot) * onehot, axis=-1))
    columns = (jnp.arange(N_DP, dtype=jnp.int32)[:, None] * CAP + slot_index).reshape(-1)
    token_of = jnp.arange(TOKENS * TOPK, dtype=jnp.int32) // TOPK
    flat_ids = route_ids.reshape(-1)
    token_table = jnp.full((EXPERTS, N_DP * CAP), TOKENS, jnp.int32).at[flat_ids, columns].set(token_of)
    weight_table = jnp.zeros((EXPERTS, N_DP * CAP), jnp.float32).at[flat_ids, columns].set(route_weight.reshape(-1))
    padded = jnp.concatenate([normed, jnp.zeros((1, D), jnp.bfloat16)], axis=0)

    def expert_step(running, expert_item):
        gate_e, up_e, down_e, token_rows, weights = expert_item
        rows = padded[token_rows]
        gate_proj = jnp.dot(rows, gate_e, preferred_element_type=jnp.float32)
        up_proj = jnp.dot(rows, up_e, preferred_element_type=jnp.float32)
        hidden_act = (jax.nn.silu(gate_proj) * up_proj).astype(jnp.bfloat16)
        expert_out = jnp.dot(hidden_act, down_e, preferred_element_type=jnp.float32).astype(jnp.bfloat16)
        expert_out = lax.optimization_barrier(expert_out).astype(jnp.float32)
        running = running.at[token_rows].add(weights[:, None] * expert_out, mode='drop')
        return (running, None)
    mixture, _ = lax.scan(expert_step, jnp.zeros((TOKENS, D), jnp.float32), (w_gate, w_up, w_down, token_table, weight_table))
    return (stream.astype(jnp.float32) + shared_out + mixture).astype(jnp.bfloat16)
```

```python
import jax
import jax.numpy as jnp
from jax import lax
from jax.sharding import PartitionSpec as P

NEGATIVE_FILL = -1e30
EPSILON = 1e-05


def normalize(rows, gain):
    values = rows.astype(jnp.float32)
    mean_square = jnp.mean(values * values, axis=-1, keepdims=True)
    return (values * lax.rsqrt(mean_square + EPSILON) * gain).astype(jnp.bfloat16)


def attend_requests(
    queries, tree_keys, tree_values, tree_allow, kv_cache, page_table, cache_len, score_scale
):

    def per_request(request_item):
        q_rows, own_keys, own_values, allow_rows, table_row, length = request_item
        kv_pages = kv_cache[table_row]
        cache_keys = kv_pages[:, 0].reshape(-1, kv_pages.shape[-1])
        cache_values = kv_pages[:, 1].reshape(-1, kv_pages.shape[-1])
        live_mask = (jnp.arange(cache_keys.shape[0], dtype=jnp.int32) < length)[None, :]
        cache_scores = (
            jnp.einsum("qd,kd->qk", q_rows, cache_keys, preferred_element_type=jnp.float32)
            * score_scale
        )
        cache_scores = jnp.where(live_mask, cache_scores, NEGATIVE_FILL)
        tree_scores = (
            jnp.einsum("qd,ud->qu", q_rows, own_keys, preferred_element_type=jnp.float32)
            * score_scale
        )
        tree_scores = jnp.where(allow_rows, tree_scores, NEGATIVE_FILL)
        row_peak = jnp.maximum(jnp.max(cache_scores, axis=1), jnp.max(tree_scores, axis=1))[:, None]
        cache_probs = jnp.where(live_mask, jnp.exp(cache_scores - row_peak), 0.0)
        tree_probs = jnp.where(allow_rows, jnp.exp(tree_scores - row_peak), 0.0)
        denom_sum = jnp.sum(cache_probs, axis=1) + jnp.sum(tree_probs, axis=1)
        weighted = jnp.dot(
            cache_probs.astype(jnp.bfloat16), cache_values, preferred_element_type=jnp.float32
        )
        weighted = weighted + jnp.dot(
            tree_probs.astype(jnp.bfloat16), own_values, preferred_element_type=jnp.float32
        )
        return (weighted / denom_sum[:, None]).astype(jnp.bfloat16)

    return lax.map(
        per_request, (queries, tree_keys, tree_values, tree_allow, page_table, cache_len)
    )


def gather_mp(block, axis):
    parts = lax.axis_size("mp")
    copies = jnp.broadcast_to(block[None], (parts,) + block.shape)
    pieces = lax.all_to_all(copies, "mp", split_axis=0, concat_axis=0, tiled=True)
    pieces = jnp.moveaxis(pieces, 0, axis)
    shape = list(block.shape)
    shape[axis] = shape[axis] * parts
    return pieces.reshape(shape)


def scatter_sum_mp(terms):
    parts = lax.axis_size("mp")
    rows, width = terms.shape
    blocks = terms.reshape(rows, parts, width // parts).transpose(1, 0, 2)
    pieces = lax.all_to_all(blocks, "mp", split_axis=0, concat_axis=0, tiled=True)
    return jnp.sum(pieces.astype(jnp.float32), axis=0)


def run_experts(rows, w_gate, w_up, w_down):
    source_count, slot_count, model_width = rows.shape
    flat_rows = rows.reshape(source_count * slot_count, model_width)
    gate_proj = jnp.dot(flat_rows, w_gate[0], preferred_element_type=jnp.float32)
    up_proj = jnp.dot(flat_rows, w_up[0], preferred_element_type=jnp.float32)
    hidden_act = (jax.nn.silu(gate_proj) * up_proj).astype(jnp.bfloat16)
    down_rows = w_down[0]
    summed = jnp.dot(
        gather_mp(hidden_act, 1),
        down_rows,
        preferred_element_type=jnp.float32,
    )
    outputs = summed.astype(jnp.bfloat16).reshape(source_count, slot_count, w_down.shape[2])
    return lax.all_to_all(outputs, "dp", split_axis=0, concat_axis=0, tiled=True)


def shared_experts(normed_rows, shared_gate, shared_up, shared_down):
    gate_total = jnp.dot(
        normed_rows,
        lax.all_gather(shared_gate, "dp", axis=0, tiled=True),
        preferred_element_type=jnp.float32,
    )
    up_total = jnp.dot(
        normed_rows,
        lax.all_gather(shared_up, "dp", axis=0, tiled=True),
        preferred_element_type=jnp.float32,
    )
    shared_hidden = (jax.nn.silu(gate_total) * up_total).astype(jnp.bfloat16)
    terms = jnp.dot(
        shared_hidden,
        lax.all_gather(shared_down, "dp", axis=1, tiled=True),
        preferred_element_type=jnp.float32,
    )
    return scatter_sum_mp(terms.astype(jnp.bfloat16))


def on_device(
    tree_query,
    new_kv,
    kv_cache,
    page_table,
    cache_len,
    tree_mask,
    out_weight,
    residual_in,
    norm_gain,
    route_ids,
    route_weight,
    w_gate,
    w_up,
    w_down,
    shared_gate,
    shared_up,
    shared_down,
):
    tok_rows = tree_query.shape[0]
    req_count = cache_len.shape[0]
    tree_len = tree_mask.shape[1]
    head_width = new_kv.shape[2]
    local_heads = tree_query.shape[1] // head_width
    score_scale = head_width ** (-0.5)
    queries = tree_query.reshape(req_count, tree_len, local_heads, head_width)
    queries = queries.transpose(0, 2, 1, 3).reshape(req_count, local_heads * tree_len, head_width)
    tree_keys = new_kv[:, 0, :].reshape(req_count, tree_len, head_width)
    tree_values = new_kv[:, 1, :].reshape(req_count, tree_len, head_width)
    tree_allow = jnp.tile(tree_mask, (1, local_heads, 1)) == 1
    attended = attend_requests(
        queries, tree_keys, tree_values, tree_allow, kv_cache, page_table, cache_len, score_scale
    )
    attended = attended.reshape(req_count, local_heads, tree_len, head_width).transpose(0, 2, 1, 3)
    attended = attended.reshape(tok_rows, local_heads * head_width)
    partial_value = jnp.dot(attended, out_weight, preferred_element_type=jnp.float32)
    model_width = residual_in.shape[1]
    quarter = model_width // lax.axis_size("mp")
    col_start = lax.axis_index("mp") * quarter
    experts = lax.axis_size("dp") * w_gate.shape[0]
    route_count = route_ids.shape[1]
    capacity = min(tok_rows, 4 * tok_rows * route_count // (3 * experts))
    expert_ids = route_ids.reshape(-1)
    onehot = (expert_ids[:, None] == jnp.arange(experts, dtype=jnp.int32)[None, :]).astype(
        jnp.int32
    )
    slot_index = jnp.sum((jnp.cumsum(onehot, axis=0) - onehot) * onehot, axis=1)
    own_residual = lax.dynamic_slice_in_dim(residual_in, col_start, quarter, 1)
    own_stream = (own_residual.astype(jnp.float32) + scatter_sum_mp(partial_value)).astype(jnp.bfloat16)
    stream = gather_mp(own_stream, 1)
    normed_rows = normalize(stream, norm_gain)
    codes = (expert_ids * capacity + slot_index).reshape(tok_rows, route_count)
    slots = jnp.arange(experts * capacity, dtype=jnp.int32)
    placing = jnp.any(codes[None, :, :] == slots[:, None, None], axis=2).astype(jnp.bfloat16)
    buffer = jnp.dot(placing, normed_rows, preferred_element_type=jnp.float32).astype(jnp.bfloat16)
    buffer = buffer.reshape(experts, capacity, normed_rows.shape[1])
    results = run_experts(
        lax.all_to_all(
            buffer,
            "dp",
            split_axis=0,
            concat_axis=0,
            tiled=True,
        ),
        w_gate,
        w_up,
        w_down,
    )
    shared_out = shared_experts(normed_rows, shared_gate, shared_up, shared_down)
    result_rows = results.reshape(experts * capacity, quarter)
    picked = (
        result_rows[expert_ids * capacity + slot_index]
        .reshape(tok_rows, route_count, quarter)
        .astype(jnp.float32)
    )
    mixture = jnp.einsum("tk,tkc->tc", route_weight, picked, precision=lax.Precision.HIGHEST)
    return (own_stream.astype(jnp.float32) + shared_out.astype(jnp.float32) + mixture).astype(
        jnp.bfloat16
    )


def solution(mesh):
    return jax.shard_map(
        on_device,
        mesh=mesh,
        in_specs=(
            P("dp", "mp"),
            P("dp", None, "mp"),
            P("dp", None, None, "mp"),
            P("dp", None),
            P("dp"),
            P("dp", None, None),
            P("mp", None),
            P("dp", None),
            P(),
            P("dp", None),
            P("dp", None),
            P("dp", None, "mp"),
            P("dp", None, "mp"),
            P("dp", None, "mp"),
            P("dp", "mp"),
            P("dp", "mp"),
            P("mp", "dp"),
        ),
        out_specs=P("dp", "mp"),
        check_vma=False,
    )
```

```python
import jax
import jax.numpy as jnp
from jax import lax
from jax.sharding import PartitionSpec as P

NEGATIVE_FILL = -1e30
EPSILON = 1e-05


def normalize(rows, gain):
    values = rows.astype(jnp.float32)
    mean_square = jnp.mean(values * values, axis=-1, keepdims=True)
    return (values * lax.rsqrt(mean_square + EPSILON) * gain).astype(jnp.bfloat16)


def attend_requests(
    queries, tree_keys, tree_values, tree_allow, kv_cache, page_table, cache_len, score_scale
):

    def per_request(request_item):
        q_rows, own_keys, own_values, allow_rows, table_row, length = request_item
        kv_pages = kv_cache[table_row]
        cache_keys = kv_pages[:, 0].reshape(-1, kv_pages.shape[-1])
        cache_values = kv_pages[:, 1].reshape(-1, kv_pages.shape[-1])
        live_mask = (jnp.arange(cache_keys.shape[0], dtype=jnp.int32) < length)[None, :]
        cache_scores = (
            jnp.einsum("qd,kd->qk", q_rows, cache_keys, preferred_element_type=jnp.float32)
            * score_scale
        )
        cache_scores = jnp.where(live_mask, cache_scores, NEGATIVE_FILL)
        tree_scores = (
            jnp.einsum("qd,ud->qu", q_rows, own_keys, preferred_element_type=jnp.float32)
            * score_scale
        )
        tree_scores = jnp.where(allow_rows, tree_scores, NEGATIVE_FILL)
        row_peak = jnp.maximum(jnp.max(cache_scores, axis=1), jnp.max(tree_scores, axis=1))[:, None]
        cache_probs = jnp.where(live_mask, jnp.exp(cache_scores - row_peak), 0.0)
        tree_probs = jnp.where(allow_rows, jnp.exp(tree_scores - row_peak), 0.0)
        denom_sum = jnp.sum(cache_probs, axis=1) + jnp.sum(tree_probs, axis=1)
        weighted = jnp.dot(
            cache_probs.astype(jnp.bfloat16), cache_values, preferred_element_type=jnp.float32
        )
        weighted = weighted + jnp.dot(
            tree_probs.astype(jnp.bfloat16), own_values, preferred_element_type=jnp.float32
        )
        return (weighted / denom_sum[:, None]).astype(jnp.bfloat16)

    return lax.map(
        per_request, (queries, tree_keys, tree_values, tree_allow, page_table, cache_len)
    )


def gather_mp(block, axis):
    parts = lax.axis_size("mp")
    copies = jnp.broadcast_to(block[None], (parts,) + block.shape)
    pieces = lax.all_to_all(copies, "mp", split_axis=0, concat_axis=0, tiled=True)
    pieces = jnp.moveaxis(pieces, 0, axis)
    shape = list(block.shape)
    shape[axis] = shape[axis] * parts
    return pieces.reshape(shape)


def scatter_sum_mp(terms):
    parts = lax.axis_size("mp")
    rows, width = terms.shape
    blocks = terms.reshape(rows, parts, width // parts).transpose(1, 0, 2)
    pieces = lax.all_to_all(blocks, "mp", split_axis=0, concat_axis=0, tiled=True)
    return jnp.sum(pieces.astype(jnp.float32), axis=0)


def run_experts(rows, w_gate, w_up, w_down):
    source_count, slot_count, model_width = rows.shape
    flat_rows = rows.reshape(source_count * slot_count, model_width)
    gate_proj = jnp.dot(flat_rows, w_gate[0], preferred_element_type=jnp.float32)
    up_proj = jnp.dot(flat_rows, w_up[0], preferred_element_type=jnp.float32)
    hidden_act = (jax.nn.silu(gate_proj) * up_proj).astype(jnp.bfloat16)
    down_rows = w_down[0]
    summed = jnp.dot(
        gather_mp(hidden_act, 1),
        down_rows,
        preferred_element_type=jnp.float32,
    )
    outputs = summed.astype(jnp.bfloat16).reshape(source_count, slot_count, w_down.shape[2])
    return lax.all_to_all(outputs, "dp", split_axis=0, concat_axis=0, tiled=True)


def shared_experts(normed_rows, shared_gate, shared_up, shared_down):
    hidden_width = shared_gate.shape[1]
    packed = jnp.concatenate([shared_gate, shared_up, shared_down.T], axis=1)
    gathered = lax.all_gather(packed, "dp", axis=0, tiled=True)
    gate_total = jnp.dot(
        normed_rows, gathered[:, :hidden_width], preferred_element_type=jnp.float32
    )
    up_total = jnp.dot(
        normed_rows, gathered[:, hidden_width : 2 * hidden_width], preferred_element_type=jnp.float32
    )
    shared_hidden = (jax.nn.silu(gate_total) * up_total).astype(jnp.bfloat16)
    terms = jnp.einsum(
        "th,dh->td",
        shared_hidden,
        gathered[:, 2 * hidden_width :],
        preferred_element_type=jnp.float32,
    )
    return scatter_sum_mp(terms.astype(jnp.bfloat16))


def on_device(
    tree_query,
    new_kv,
    kv_cache,
    page_table,
    cache_len,
    tree_mask,
    out_weight,
    residual_in,
    norm_gain,
    route_ids,
    route_weight,
    w_gate,
    w_up,
    w_down,
    shared_gate,
    shared_up,
    shared_down,
):
    tok_rows = tree_query.shape[0]
    req_count = cache_len.shape[0]
    tree_len = tree_mask.shape[1]
    head_width = new_kv.shape[2]
    local_heads = tree_query.shape[1] // head_width
    score_scale = head_width ** (-0.5)
    queries = tree_query.reshape(req_count, tree_len, local_heads, head_width)
    queries = queries.transpose(0, 2, 1, 3).reshape(req_count, local_heads * tree_len, head_width)
    tree_keys = new_kv[:, 0, :].reshape(req_count, tree_len, head_width)
    tree_values = new_kv[:, 1, :].reshape(req_count, tree_len, head_width)
    tree_allow = jnp.tile(tree_mask, (1, local_heads, 1)) == 1
    attended = attend_requests(
        queries, tree_keys, tree_values, tree_allow, kv_cache, page_table, cache_len, score_scale
    )
    attended = attended.reshape(req_count, local_heads, tree_len, head_width).transpose(0, 2, 1, 3)
    attended = attended.reshape(tok_rows, local_heads * head_width)
    partial_value = jnp.dot(attended, out_weight, preferred_element_type=jnp.float32)
    model_width = residual_in.shape[1]
    quarter = model_width // lax.axis_size("mp")
    col_start = lax.axis_index("mp") * quarter
    experts = lax.axis_size("dp") * w_gate.shape[0]
    route_count = route_ids.shape[1]
    capacity = min(tok_rows, 4 * tok_rows * route_count // (3 * experts))
    expert_ids = route_ids.reshape(-1)
    onehot = (expert_ids[:, None] == jnp.arange(experts, dtype=jnp.int32)[None, :]).astype(
        jnp.int32
    )
    slot_index = jnp.sum((jnp.cumsum(onehot, axis=0) - onehot) * onehot, axis=1)
    own_residual = lax.dynamic_slice_in_dim(residual_in, col_start, quarter, 1)
    own_stream = (own_residual.astype(jnp.float32) + scatter_sum_mp(partial_value)).astype(jnp.bfloat16)
    stream = gather_mp(own_stream, 1)
    normed_rows = normalize(stream, norm_gain)
    codes = (expert_ids * capacity + slot_index).reshape(tok_rows, route_count)
    slots = jnp.arange(experts * capacity, dtype=jnp.int32)
    placing = jnp.any(codes[None, :, :] == slots[:, None, None], axis=2).astype(jnp.bfloat16)
    buffer = jnp.dot(placing, normed_rows, preferred_element_type=jnp.float32).astype(jnp.bfloat16)
    buffer = buffer.reshape(experts, capacity, normed_rows.shape[1])
    results = run_experts(
        lax.all_to_all(
            buffer,
            "dp",
            split_axis=0,
            concat_axis=0,
            tiled=True,
        ),
        w_gate,
        w_up,
        w_down,
    )
    shared_out = shared_experts(normed_rows, shared_gate, shared_up, shared_down)
    result_rows = results.reshape(experts * capacity, quarter)
    picked = (
        result_rows[expert_ids * capacity + slot_index]
        .reshape(tok_rows, route_count, quarter)
        .astype(jnp.float32)
    )
    mixture = jnp.einsum("tk,tkc->tc", route_weight, picked, precision=lax.Precision.HIGHEST)
    return (own_stream.astype(jnp.float32) + shared_out.astype(jnp.float32) + mixture).astype(
        jnp.bfloat16
    )


def solution(mesh):
    return jax.shard_map(
        on_device,
        mesh=mesh,
        in_specs=(
            P("dp", "mp"),
            P("dp", None, "mp"),
            P("dp", None, None, "mp"),
            P("dp", None),
            P("dp"),
            P("dp", None, None),
            P("mp", None),
            P("dp", None),
            P(),
            P("dp", None),
            P("dp", None),
            P("dp", None, "mp"),
            P("dp", None, "mp"),
            P("dp", None, "mp"),
            P("dp", "mp"),
            P("dp", "mp"),
            P("mp", "dp"),
        ),
        out_specs=P("dp", "mp"),
        check_vma=False,
    )
```

```python
import jax
import jax.numpy as jnp
from jax import lax
from jax.sharding import PartitionSpec as P

NEGATIVE_FILL = -1e30
EPSILON = 1e-05


def normalize(rows, gain):
    values = rows.astype(jnp.float32)
    mean_square = jnp.mean(values * values, axis=-1, keepdims=True)
    return (values * lax.rsqrt(mean_square + EPSILON) * gain).astype(jnp.bfloat16)


def attend_requests(
    queries, tree_keys, tree_values, tree_allow, kv_cache, page_table, cache_len, score_scale
):

    def per_request(request_item):
        q_rows, own_keys, own_values, allow_rows, table_row, length = request_item
        kv_pages = kv_cache[table_row]
        cache_keys = kv_pages[:, 0].reshape(-1, kv_pages.shape[-1])
        cache_values = kv_pages[:, 1].reshape(-1, kv_pages.shape[-1])
        live_mask = (jnp.arange(cache_keys.shape[0], dtype=jnp.int32) < length)[None, :]
        cache_scores = (
            jnp.einsum("qd,kd->qk", q_rows, cache_keys, preferred_element_type=jnp.float32)
            * score_scale
        )
        cache_scores = jnp.where(live_mask, cache_scores, NEGATIVE_FILL)
        tree_scores = (
            jnp.einsum("qd,ud->qu", q_rows, own_keys, preferred_element_type=jnp.float32)
            * score_scale
        )
        tree_scores = jnp.where(allow_rows, tree_scores, NEGATIVE_FILL)
        row_peak = jnp.maximum(jnp.max(cache_scores, axis=1), jnp.max(tree_scores, axis=1))[:, None]
        cache_probs = jnp.where(live_mask, jnp.exp(cache_scores - row_peak), 0.0)
        tree_probs = jnp.where(allow_rows, jnp.exp(tree_scores - row_peak), 0.0)
        denom_sum = jnp.sum(cache_probs, axis=1) + jnp.sum(tree_probs, axis=1)
        weighted = jnp.dot(
            cache_probs.astype(jnp.bfloat16), cache_values, preferred_element_type=jnp.float32
        )
        weighted = weighted + jnp.dot(
            tree_probs.astype(jnp.bfloat16), own_values, preferred_element_type=jnp.float32
        )
        return (weighted / denom_sum[:, None]).astype(jnp.bfloat16)

    return lax.map(
        per_request, (queries, tree_keys, tree_values, tree_allow, page_table, cache_len)
    )


def gather_mp(block, axis):
    parts = lax.axis_size("mp")
    copies = jnp.broadcast_to(block[None], (parts,) + block.shape)
    pieces = lax.all_to_all(copies, "mp", split_axis=0, concat_axis=0, tiled=True)
    pieces = jnp.moveaxis(pieces, 0, axis)
    shape = list(block.shape)
    shape[axis] = shape[axis] * parts
    return pieces.reshape(shape)


def scatter_sum_mp(terms):
    parts = lax.axis_size("mp")
    rows, width = terms.shape
    blocks = terms.reshape(rows, parts, width // parts).transpose(1, 0, 2)
    pieces = lax.all_to_all(blocks, "mp", split_axis=0, concat_axis=0, tiled=True)
    return jnp.sum(pieces.astype(jnp.float32), axis=0)


def run_experts(rows, w_gate, w_up, w_down):
    source_count, slot_count, model_width = rows.shape
    flat_rows = rows.reshape(source_count * slot_count, model_width)
    gate_proj = jnp.dot(flat_rows, w_gate[0], preferred_element_type=jnp.float32)
    up_proj = jnp.dot(flat_rows, w_up[0], preferred_element_type=jnp.float32)
    hidden_act = (jax.nn.silu(gate_proj) * up_proj).astype(jnp.bfloat16)
    down_rows = w_down[0]
    summed = jnp.dot(
        gather_mp(hidden_act, 1),
        down_rows,
        preferred_element_type=jnp.float32,
    )
    outputs = summed.astype(jnp.bfloat16).reshape(source_count, slot_count, w_down.shape[2])
    return lax.all_to_all(outputs, "dp", split_axis=0, concat_axis=0, tiled=True)


def shared_experts(normed_rows, shared_gate, shared_up, shared_down):
    hidden_width = shared_gate.shape[1]
    packed = jnp.concatenate([shared_gate, shared_up, shared_down.T], axis=1)
    gathered = lax.all_gather(packed, "dp", axis=0, tiled=True)
    gate_total = jnp.dot(
        normed_rows, gathered[:, :hidden_width], preferred_element_type=jnp.float32
    )
    up_total = jnp.dot(
        normed_rows, gathered[:, hidden_width : 2 * hidden_width], preferred_element_type=jnp.float32
    )
    shared_hidden = (jax.nn.silu(gate_total) * up_total).astype(jnp.bfloat16)
    terms = jnp.einsum(
        "th,dh->td",
        shared_hidden,
        gathered[:, 2 * hidden_width :],
        preferred_element_type=jnp.float32,
    )
    return scatter_sum_mp(terms.astype(jnp.bfloat16))


def on_device(
    tree_query,
    new_kv,
    kv_cache,
    page_table,
    cache_len,
    tree_mask,
    out_weight,
    residual_in,
    norm_gain,
    route_ids,
    route_weight,
    w_gate,
    w_up,
    w_down,
    shared_gate,
    shared_up,
    shared_down,
):
    tok_rows = tree_query.shape[0]
    req_count = cache_len.shape[0]
    tree_len = tree_mask.shape[1]
    head_width = new_kv.shape[2]
    local_heads = tree_query.shape[1] // head_width
    score_scale = head_width ** (-0.5)
    queries = tree_query.reshape(req_count, tree_len, local_heads, head_width)
    queries = queries.transpose(0, 2, 1, 3).reshape(req_count, local_heads * tree_len, head_width)
    tree_keys = new_kv[:, 0, :].reshape(req_count, tree_len, head_width)
    tree_values = new_kv[:, 1, :].reshape(req_count, tree_len, head_width)
    tree_allow = jnp.tile(tree_mask, (1, local_heads, 1)) == 1
    attended = attend_requests(
        queries, tree_keys, tree_values, tree_allow, kv_cache, page_table, cache_len, score_scale
    )
    attended = attended.reshape(req_count, local_heads, tree_len, head_width).transpose(0, 2, 1, 3)
    attended = attended.reshape(tok_rows, local_heads * head_width)
    partial_value = jnp.dot(attended, out_weight, preferred_element_type=jnp.float32)
    model_width = residual_in.shape[1]
    quarter = model_width // lax.axis_size("mp")
    col_start = lax.axis_index("mp") * quarter
    experts = lax.axis_size("dp") * w_gate.shape[0]
    route_count = route_ids.shape[1]
    capacity = min(tok_rows, 4 * tok_rows * route_count // (3 * experts))
    expert_ids = route_ids.reshape(-1)
    onehot = (expert_ids[:, None] == jnp.arange(experts, dtype=jnp.int32)[None, :]).astype(
        jnp.int32
    )
    slot_index = jnp.sum((jnp.cumsum(onehot, axis=0) - onehot) * onehot, axis=1)
    own_residual = lax.dynamic_slice_in_dim(residual_in, col_start, quarter, 1)
    own_stream = (own_residual.astype(jnp.float32) + scatter_sum_mp(partial_value)).astype(jnp.bfloat16)
    stream = gather_mp(own_stream, 1)
    normed_rows = normalize(stream, norm_gain)
    codes = (expert_ids * capacity + slot_index).reshape(tok_rows, route_count)
    slots = jnp.arange(experts * capacity, dtype=jnp.int32)
    placing = jnp.any(codes[None, :, :] == slots[:, None, None], axis=2).astype(jnp.bfloat16)
    own_normed = lax.dynamic_slice_in_dim(normed_rows, col_start, quarter, 1)
    buffer = jnp.dot(placing, own_normed, preferred_element_type=jnp.float32).astype(jnp.bfloat16)
    buffer = buffer.reshape(experts, capacity, quarter)
    received = lax.all_to_all(buffer, "dp", split_axis=0, concat_axis=0, tiled=True)
    results = run_experts(
        gather_mp(received.reshape(experts * capacity, quarter), 1).reshape(
            experts, capacity, model_width
        ),
        w_gate,
        w_up,
        w_down,
    )
    shared_out = shared_experts(normed_rows, shared_gate, shared_up, shared_down)
    result_rows = results.reshape(experts * capacity, quarter)
    picked = (
        result_rows[expert_ids * capacity + slot_index]
        .reshape(tok_rows, route_count, quarter)
        .astype(jnp.float32)
    )
    mixture = jnp.einsum("tk,tkc->tc", route_weight, picked, precision=lax.Precision.HIGHEST)
    return (own_stream.astype(jnp.float32) + shared_out.astype(jnp.float32) + mixture).astype(
        jnp.bfloat16
    )


def solution(mesh):
    return jax.shard_map(
        on_device,
        mesh=mesh,
        in_specs=(
            P("dp", "mp"),
            P("dp", None, "mp"),
            P("dp", None, None, "mp"),
            P("dp", None),
            P("dp"),
            P("dp", None, None),
            P("mp", None),
            P("dp", None),
            P(),
            P("dp", None),
            P("dp", None),
            P("dp", None, "mp"),
            P("dp", None, "mp"),
            P("dp", None, "mp"),
            P("dp", "mp"),
            P("dp", "mp"),
            P("mp", "dp"),
        ),
        out_specs=P("dp", "mp"),
        check_vma=False,
    )
```

```python
import jax
import jax.numpy as jnp
from jax import lax
from jax.sharding import PartitionSpec as P

NEGATIVE_FILL = -1e30
EPSILON = 1e-05


def normalize(rows, gain):
    values = rows.astype(jnp.float32)
    mean_square = jnp.mean(values * values, axis=-1, keepdims=True)
    return (values * lax.rsqrt(mean_square + EPSILON) * gain).astype(jnp.bfloat16)


def attend_requests(
    queries, tree_keys, tree_values, tree_allow, kv_cache, page_table, cache_len, score_scale
):

    def per_request(request_item):
        q_rows, own_keys, own_values, allow_rows, table_row, length = request_item
        kv_pages = kv_cache[table_row]
        cache_keys = kv_pages[:, 0].reshape(-1, kv_pages.shape[-1])
        cache_values = kv_pages[:, 1].reshape(-1, kv_pages.shape[-1])
        live_mask = (jnp.arange(cache_keys.shape[0], dtype=jnp.int32) < length)[None, :]
        cache_scores = (
            jnp.einsum("qd,kd->qk", q_rows, cache_keys, preferred_element_type=jnp.float32)
            * score_scale
        )
        cache_scores = jnp.where(live_mask, cache_scores, NEGATIVE_FILL)
        tree_scores = (
            jnp.einsum("qd,ud->qu", q_rows, own_keys, preferred_element_type=jnp.float32)
            * score_scale
        )
        tree_scores = jnp.where(allow_rows, tree_scores, NEGATIVE_FILL)
        row_peak = jnp.maximum(jnp.max(cache_scores, axis=1), jnp.max(tree_scores, axis=1))[:, None]
        cache_probs = jnp.where(live_mask, jnp.exp(cache_scores - row_peak), 0.0)
        tree_probs = jnp.where(allow_rows, jnp.exp(tree_scores - row_peak), 0.0)
        denom_sum = jnp.sum(cache_probs, axis=1) + jnp.sum(tree_probs, axis=1)
        weighted = jnp.dot(
            cache_probs.astype(jnp.bfloat16), cache_values, preferred_element_type=jnp.float32
        )
        weighted = weighted + jnp.dot(
            tree_probs.astype(jnp.bfloat16), own_values, preferred_element_type=jnp.float32
        )
        return (weighted / denom_sum[:, None]).astype(jnp.bfloat16)

    return lax.map(
        per_request, (queries, tree_keys, tree_values, tree_allow, page_table, cache_len)
    )


def gather_mp(block, axis):
    parts = lax.axis_size("mp")
    copies = jnp.broadcast_to(block[None], (parts,) + block.shape)
    pieces = lax.all_to_all(copies, "mp", split_axis=0, concat_axis=0, tiled=True)
    pieces = jnp.moveaxis(pieces, 0, axis)
    shape = list(block.shape)
    shape[axis] = shape[axis] * parts
    return pieces.reshape(shape)


def scatter_sum_mp(terms):
    parts = lax.axis_size("mp")
    rows, width = terms.shape
    blocks = terms.reshape(rows, parts, width // parts).transpose(1, 0, 2)
    pieces = lax.all_to_all(blocks, "mp", split_axis=0, concat_axis=0, tiled=True)
    return jnp.sum(pieces.astype(jnp.float32), axis=0)


def run_experts(rows, w_gate, w_up, w_down):
    source_count, slot_count, model_width = rows.shape
    flat_rows = rows.reshape(source_count * slot_count, model_width)
    gate_proj = jnp.dot(flat_rows, w_gate[0], preferred_element_type=jnp.float32)
    up_proj = jnp.dot(flat_rows, w_up[0], preferred_element_type=jnp.float32)
    hidden_act = (jax.nn.silu(gate_proj) * up_proj).astype(jnp.bfloat16)
    down_rows = w_down[0]
    summed = jnp.dot(
        gather_mp(hidden_act, 1),
        down_rows,
        preferred_element_type=jnp.float32,
    )
    outputs = summed.astype(jnp.bfloat16).reshape(source_count, slot_count, w_down.shape[2])
    return lax.all_to_all(outputs, "dp", split_axis=0, concat_axis=0, tiled=True)


def shared_experts(normed_rows, shared_gate, shared_up, shared_down):
    hidden_width = shared_gate.shape[1]
    packed = jnp.concatenate([shared_gate, shared_up, shared_down.T], axis=1)
    gathered = lax.all_gather(packed, "dp", axis=0, tiled=True)
    gate_total = jnp.dot(
        normed_rows, gathered[:, :hidden_width], preferred_element_type=jnp.float32
    )
    up_total = jnp.dot(
        normed_rows, gathered[:, hidden_width : 2 * hidden_width], preferred_element_type=jnp.float32
    )
    shared_hidden = (jax.nn.silu(gate_total) * up_total).astype(jnp.bfloat16)
    terms = jnp.einsum(
        "th,dh->td",
        shared_hidden,
        gathered[:, 2 * hidden_width :],
        preferred_element_type=jnp.float32,
    )
    return scatter_sum_mp(terms.astype(jnp.bfloat16))


def on_device(
    tree_query,
    new_kv,
    kv_cache,
    page_table,
    cache_len,
    tree_mask,
    out_weight,
    residual_in,
    norm_gain,
    route_ids,
    route_weight,
    w_gate,
    w_up,
    w_down,
    shared_gate,
    shared_up,
    shared_down,
):
    tok_rows = tree_query.shape[0]
    req_count = cache_len.shape[0]
    tree_len = tree_mask.shape[1]
    head_width = new_kv.shape[2]
    local_heads = tree_query.shape[1] // head_width
    score_scale = head_width ** (-0.5)
    queries = tree_query.reshape(req_count, tree_len, local_heads, head_width)
    queries = queries.transpose(0, 2, 1, 3).reshape(req_count, local_heads * tree_len, head_width)
    tree_keys = new_kv[:, 0, :].reshape(req_count, tree_len, head_width)
    tree_values = new_kv[:, 1, :].reshape(req_count, tree_len, head_width)
    tree_allow = jnp.tile(tree_mask, (1, local_heads, 1)) == 1
    attended = attend_requests(
        queries, tree_keys, tree_values, tree_allow, kv_cache, page_table, cache_len, score_scale
    )
    attended = attended.reshape(req_count, local_heads, tree_len, head_width).transpose(0, 2, 1, 3)
    attended = attended.reshape(tok_rows, local_heads * head_width)
    partial_value = jnp.dot(attended, out_weight, preferred_element_type=jnp.float32)
    model_width = residual_in.shape[1]
    quarter = model_width // lax.axis_size("mp")
    col_start = lax.axis_index("mp") * quarter
    experts = lax.axis_size("dp") * w_gate.shape[0]
    route_count = route_ids.shape[1]
    capacity = min(tok_rows, 4 * tok_rows * route_count // (3 * experts))
    expert_ids = route_ids.reshape(-1)
    onehot = (expert_ids[:, None] == jnp.arange(experts, dtype=jnp.int32)[None, :]).astype(
        jnp.int32
    )
    slot_index = jnp.sum((jnp.cumsum(onehot, axis=0) - onehot) * onehot, axis=1)
    own_residual = lax.dynamic_slice_in_dim(residual_in, col_start, quarter, 1)
    own_stream = (own_residual.astype(jnp.float32) + scatter_sum_mp(partial_value)).astype(jnp.bfloat16)
    stream = gather_mp(own_stream, 1)
    normed_rows = normalize(stream, norm_gain)
    codes = (expert_ids * capacity + slot_index).reshape(tok_rows, route_count)
    slots = jnp.arange(experts * capacity, dtype=jnp.int32)
    placing = jnp.any(codes[None, :, :] == slots[:, None, None], axis=2).astype(jnp.bfloat16)
    parts = lax.axis_size("mp")
    mp_index = lax.axis_index("mp")
    normed_blocks = normed_rows.reshape(tok_rows, parts, quarter)
    pair = jnp.take(normed_blocks, (mp_index + jnp.arange(2)) % parts, axis=1)
    pair = pair.reshape(tok_rows, 2 * quarter)
    buffer = jnp.dot(placing, pair, preferred_element_type=jnp.float32).astype(jnp.bfloat16)
    buffer = buffer.reshape(experts, capacity, 2 * quarter)
    received = lax.all_to_all(buffer, "dp", split_axis=0, concat_axis=0, tiled=True)
    received = received.reshape(experts * capacity, 2, quarter)
    from_left = lax.ppermute(
        received[:, 0], "mp", [(k, (k + 1) % parts) for k in range(parts)]
    )
    from_right = lax.ppermute(
        received[:, 1], "mp", [(k, (k - 1) % parts) for k in range(parts)]
    )
    rotated = jnp.concatenate(
        [received.reshape(experts * capacity, 2 * quarter), from_right, from_left], axis=1
    )
    full_rows = jnp.roll(rotated, mp_index * quarter, axis=1)
    results = run_experts(
        full_rows.reshape(experts, capacity, model_width),
        w_gate,
        w_up,
        w_down,
    )
    shared_out = shared_experts(normed_rows, shared_gate, shared_up, shared_down)
    result_rows = results.reshape(experts * capacity, quarter)
    picked = (
        result_rows[expert_ids * capacity + slot_index]
        .reshape(tok_rows, route_count, quarter)
        .astype(jnp.float32)
    )
    mixture = jnp.einsum("tk,tkc->tc", route_weight, picked, precision=lax.Precision.HIGHEST)
    return (own_stream.astype(jnp.float32) + shared_out.astype(jnp.float32) + mixture).astype(
        jnp.bfloat16
    )


def solution(mesh):
    return jax.shard_map(
        on_device,
        mesh=mesh,
        in_specs=(
            P("dp", "mp"),
            P("dp", None, "mp"),
            P("dp", None, None, "mp"),
            P("dp", None),
            P("dp"),
            P("dp", None, None),
            P("mp", None),
            P("dp", None),
            P(),
            P("dp", None),
            P("dp", None),
            P("dp", None, "mp"),
            P("dp", None, "mp"),
            P("dp", None, "mp"),
            P("dp", "mp"),
            P("dp", "mp"),
            P("mp", "dp"),
        ),
        out_specs=P("dp", "mp"),
        check_vma=False,
    )
```

```python
import jax
import jax.numpy as jnp
from jax import lax
from jax.sharding import PartitionSpec as P

NEGATIVE_FILL = -1e30
EPSILON = 1e-05


def normalize(rows, gain):
    values = rows.astype(jnp.float32)
    mean_square = jnp.mean(values * values, axis=-1, keepdims=True)
    return (values * lax.rsqrt(mean_square + EPSILON) * gain).astype(jnp.bfloat16)


def attend_requests(
    queries, tree_keys, tree_values, tree_allow, kv_cache, page_table, cache_len, score_scale
):

    def per_request(request_item):
        q_rows, own_keys, own_values, allow_rows, table_row, length = request_item
        kv_pages = kv_cache[table_row]
        cache_keys = kv_pages[:, 0].reshape(-1, kv_pages.shape[-1])
        cache_values = kv_pages[:, 1].reshape(-1, kv_pages.shape[-1])
        live_mask = (jnp.arange(cache_keys.shape[0], dtype=jnp.int32) < length)[None, :]
        cache_scores = (
            jnp.einsum("qd,kd->qk", q_rows, cache_keys, preferred_element_type=jnp.float32)
            * score_scale
        )
        cache_scores = jnp.where(live_mask, cache_scores, NEGATIVE_FILL)
        tree_scores = (
            jnp.einsum("qd,ud->qu", q_rows, own_keys, preferred_element_type=jnp.float32)
            * score_scale
        )
        tree_scores = jnp.where(allow_rows, tree_scores, NEGATIVE_FILL)
        row_peak = jnp.maximum(jnp.max(cache_scores, axis=1), jnp.max(tree_scores, axis=1))[:, None]
        cache_probs = jnp.where(live_mask, jnp.exp(cache_scores - row_peak), 0.0)
        tree_probs = jnp.where(allow_rows, jnp.exp(tree_scores - row_peak), 0.0)
        denom_sum = jnp.sum(cache_probs, axis=1) + jnp.sum(tree_probs, axis=1)
        weighted = jnp.dot(
            cache_probs.astype(jnp.bfloat16), cache_values, preferred_element_type=jnp.float32
        )
        weighted = weighted + jnp.dot(
            tree_probs.astype(jnp.bfloat16), own_values, preferred_element_type=jnp.float32
        )
        return (weighted / denom_sum[:, None]).astype(jnp.bfloat16)

    return lax.map(
        per_request, (queries, tree_keys, tree_values, tree_allow, page_table, cache_len)
    )


def gather_mp(block, axis):
    parts = lax.axis_size("mp")
    copies = jnp.broadcast_to(block[None], (parts,) + block.shape)
    pieces = lax.all_to_all(copies, "mp", split_axis=0, concat_axis=0, tiled=True)
    pieces = jnp.moveaxis(pieces, 0, axis)
    shape = list(block.shape)
    shape[axis] = shape[axis] * parts
    return pieces.reshape(shape)


def scatter_sum_mp(terms):
    parts = lax.axis_size("mp")
    rows, width = terms.shape
    blocks = terms.reshape(rows, parts, width // parts).transpose(1, 0, 2)
    pieces = lax.all_to_all(blocks, "mp", split_axis=0, concat_axis=0, tiled=True)
    return jnp.sum(pieces.astype(jnp.float32), axis=0)


def run_experts(rows, w_gate, w_up, w_down):
    source_count, slot_count, model_width = rows.shape
    flat_rows = rows.reshape(source_count * slot_count, model_width)
    gate_proj = jnp.dot(flat_rows, w_gate[0], preferred_element_type=jnp.float32)
    up_proj = jnp.dot(flat_rows, w_up[0], preferred_element_type=jnp.float32)
    hidden_act = (jax.nn.silu(gate_proj) * up_proj).astype(jnp.bfloat16)
    down_rows = w_down[0]
    summed = jnp.dot(
        gather_mp(hidden_act, 1),
        down_rows,
        preferred_element_type=jnp.float32,
    )
    outputs = summed.astype(jnp.bfloat16).reshape(source_count, slot_count, w_down.shape[2])
    return lax.all_to_all(outputs, "dp", split_axis=0, concat_axis=0, tiled=True)


def shared_experts(normed_rows, shared_gate, shared_up, shared_down, after):
    hidden_width = shared_gate.shape[1]
    packed = jnp.concatenate([shared_gate, shared_up, shared_down.T], axis=1)
    packed, after = lax.optimization_barrier((packed, after))
    gathered = lax.all_gather(packed, "dp", axis=0, tiled=True)
    gate_total = jnp.dot(
        normed_rows, gathered[:, :hidden_width], preferred_element_type=jnp.float32
    )
    up_total = jnp.dot(
        normed_rows, gathered[:, hidden_width : 2 * hidden_width], preferred_element_type=jnp.float32
    )
    shared_hidden = (jax.nn.silu(gate_total) * up_total).astype(jnp.bfloat16)
    terms = jnp.einsum(
        "th,dh->td",
        shared_hidden,
        gathered[:, 2 * hidden_width :],
        preferred_element_type=jnp.float32,
    )
    return scatter_sum_mp(terms.astype(jnp.bfloat16))


def on_device(
    tree_query,
    new_kv,
    kv_cache,
    page_table,
    cache_len,
    tree_mask,
    out_weight,
    residual_in,
    norm_gain,
    route_ids,
    route_weight,
    w_gate,
    w_up,
    w_down,
    shared_gate,
    shared_up,
    shared_down,
):
    tok_rows = tree_query.shape[0]
    req_count = cache_len.shape[0]
    tree_len = tree_mask.shape[1]
    head_width = new_kv.shape[2]
    local_heads = tree_query.shape[1] // head_width
    score_scale = head_width ** (-0.5)
    queries = tree_query.reshape(req_count, tree_len, local_heads, head_width)
    queries = queries.transpose(0, 2, 1, 3).reshape(req_count, local_heads * tree_len, head_width)
    tree_keys = new_kv[:, 0, :].reshape(req_count, tree_len, head_width)
    tree_values = new_kv[:, 1, :].reshape(req_count, tree_len, head_width)
    tree_allow = jnp.tile(tree_mask, (1, local_heads, 1)) == 1
    attended = attend_requests(
        queries, tree_keys, tree_values, tree_allow, kv_cache, page_table, cache_len, score_scale
    )
    attended = attended.reshape(req_count, local_heads, tree_len, head_width).transpose(0, 2, 1, 3)
    attended = attended.reshape(tok_rows, local_heads * head_width)
    partial_value = jnp.dot(attended, out_weight, preferred_element_type=jnp.float32)
    model_width = residual_in.shape[1]
    quarter = model_width // lax.axis_size("mp")
    col_start = lax.axis_index("mp") * quarter
    experts = lax.axis_size("dp") * w_gate.shape[0]
    route_count = route_ids.shape[1]
    capacity = min(tok_rows, 4 * tok_rows * route_count // (3 * experts))
    expert_ids = route_ids.reshape(-1)
    onehot = (expert_ids[:, None] == jnp.arange(experts, dtype=jnp.int32)[None, :]).astype(
        jnp.int32
    )
    slot_index = jnp.sum((jnp.cumsum(onehot, axis=0) - onehot) * onehot, axis=1)
    own_residual = lax.dynamic_slice_in_dim(residual_in, col_start, quarter, 1)
    own_stream = (own_residual.astype(jnp.float32) + scatter_sum_mp(partial_value)).astype(jnp.bfloat16)
    stream = gather_mp(own_stream, 1)
    normed_rows = normalize(stream, norm_gain)
    codes = (expert_ids * capacity + slot_index).reshape(tok_rows, route_count)
    slots = jnp.arange(experts * capacity, dtype=jnp.int32)
    placing = jnp.any(codes[None, :, :] == slots[:, None, None], axis=2).astype(jnp.bfloat16)
    own_normed = lax.dynamic_slice_in_dim(normed_rows, col_start, quarter, 1)
    buffer = jnp.dot(placing, own_normed, preferred_element_type=jnp.float32).astype(jnp.bfloat16)
    buffer = buffer.reshape(experts, capacity, quarter)
    received = lax.all_to_all(buffer, "dp", split_axis=0, concat_axis=0, tiled=True)
    results = run_experts(
        gather_mp(received.reshape(experts * capacity, quarter), 1).reshape(
            experts, capacity, model_width
        ),
        w_gate,
        w_up,
        w_down,
    )
    shared_out = shared_experts(normed_rows, shared_gate, shared_up, shared_down, received)
    result_rows = results.reshape(experts * capacity, quarter)
    picked = (
        result_rows[expert_ids * capacity + slot_index]
        .reshape(tok_rows, route_count, quarter)
        .astype(jnp.float32)
    )
    mixture = jnp.einsum("tk,tkc->tc", route_weight, picked, precision=lax.Precision.HIGHEST)
    return (own_stream.astype(jnp.float32) + shared_out.astype(jnp.float32) + mixture).astype(
        jnp.bfloat16
    )


def solution(mesh):
    return jax.shard_map(
        on_device,
        mesh=mesh,
        in_specs=(
            P("dp", "mp"),
            P("dp", None, "mp"),
            P("dp", None, None, "mp"),
            P("dp", None),
            P("dp"),
            P("dp", None, None),
            P("mp", None),
            P("dp", None),
            P(),
            P("dp", None),
            P("dp", None),
            P("dp", None, "mp"),
            P("dp", None, "mp"),
            P("dp", None, "mp"),
            P("dp", "mp"),
            P("dp", "mp"),
            P("mp", "dp"),
        ),
        out_specs=P("dp", "mp"),
        check_vma=False,
    )
```

```python
import jax
import jax.numpy as jnp
from jax import lax
from jax.sharding import PartitionSpec as P

NEGATIVE_FILL = -1e30
EPSILON = 1e-05


def normalize(rows, gain):
    values = rows.astype(jnp.float32)
    mean_square = jnp.mean(values * values, axis=-1, keepdims=True)
    return (values * lax.rsqrt(mean_square + EPSILON) * gain).astype(jnp.bfloat16)


def attend_requests(
    queries, tree_keys, tree_values, tree_allow, kv_cache, page_table, cache_len, score_scale
):
    pool_pages, _, page_rows, head_width = kv_cache.shape
    pool_keys = kv_cache[:, 0].reshape(pool_pages * page_rows, head_width)
    pool_values = kv_cache[:, 1].reshape(pool_pages * page_rows, head_width)
    page_start = jnp.arange(page_table.shape[1], dtype=jnp.int32) * page_rows
    rows_left = cache_len[:, None] - page_start[None, :]
    live_rows = jnp.where(rows_left > 0, jnp.minimum(rows_left, page_rows), 0)
    slot_ids = jnp.arange(pool_pages, dtype=jnp.int32)
    owns = page_table[:, :, None] == slot_ids[None, None, :]
    slot_rows = jnp.sum(jnp.where(owns, live_rows[:, :, None], 0), axis=1)
    row_ids = jnp.arange(page_rows, dtype=jnp.int32)
    live_mask = (row_ids[None, None, :] < slot_rows[:, :, None]).reshape(
        cache_len.shape[0], 1, pool_pages * page_rows
    )
    cache_scores = (
        jnp.einsum("rqd,kd->rqk", queries, pool_keys, preferred_element_type=jnp.float32)
        * score_scale
    )
    cache_scores = jnp.where(live_mask, cache_scores, NEGATIVE_FILL)
    tree_scores = (
        jnp.einsum("rqd,rud->rqu", queries, tree_keys, preferred_element_type=jnp.float32)
        * score_scale
    )
    tree_scores = jnp.where(tree_allow, tree_scores, NEGATIVE_FILL)
    row_peak = jnp.maximum(jnp.max(cache_scores, axis=2), jnp.max(tree_scores, axis=2))[..., None]
    cache_probs = jnp.where(live_mask, jnp.exp(cache_scores - row_peak), 0.0)
    tree_probs = jnp.where(tree_allow, jnp.exp(tree_scores - row_peak), 0.0)
    denom_sum = jnp.sum(cache_probs, axis=2) + jnp.sum(tree_probs, axis=2)
    weighted = jnp.einsum(
        "rqk,kd->rqd", cache_probs.astype(jnp.bfloat16), pool_values,
        preferred_element_type=jnp.float32,
    )
    weighted = weighted + jnp.einsum(
        "rqu,rud->rqd", tree_probs.astype(jnp.bfloat16), tree_values,
        preferred_element_type=jnp.float32,
    )
    return (weighted / denom_sum[..., None]).astype(jnp.bfloat16)


def gather_mp(block, axis):
    parts = lax.axis_size("mp")
    copies = jnp.broadcast_to(block[None], (parts,) + block.shape)
    pieces = lax.all_to_all(copies, "mp", split_axis=0, concat_axis=0, tiled=True)
    pieces = jnp.moveaxis(pieces, 0, axis)
    shape = list(block.shape)
    shape[axis] = shape[axis] * parts
    return pieces.reshape(shape)


def scatter_sum_mp(terms):
    parts = lax.axis_size("mp")
    rows, width = terms.shape
    blocks = terms.reshape(rows, parts, width // parts).transpose(1, 0, 2)
    pieces = lax.all_to_all(blocks, "mp", split_axis=0, concat_axis=0, tiled=True)
    return jnp.sum(pieces.astype(jnp.float32), axis=0)


def run_experts(rows, w_gate, w_up, w_down):
    source_count, slot_count, model_width = rows.shape
    flat_rows = rows.reshape(source_count * slot_count, model_width)
    gate_proj = jnp.dot(flat_rows, w_gate[0], preferred_element_type=jnp.float32)
    up_proj = jnp.dot(flat_rows, w_up[0], preferred_element_type=jnp.float32)
    hidden_act = (jax.nn.silu(gate_proj) * up_proj).astype(jnp.bfloat16)
    down_rows = w_down[0]
    summed = jnp.dot(
        gather_mp(hidden_act, 1),
        down_rows,
        preferred_element_type=jnp.float32,
    )
    outputs = summed.astype(jnp.bfloat16).reshape(source_count, slot_count, w_down.shape[2])
    return lax.all_to_all(outputs, "dp", split_axis=0, concat_axis=0, tiled=True)


def shared_experts(normed_rows, shared_gate, shared_up, shared_down, after):
    hidden_width = shared_gate.shape[1]
    packed = jnp.concatenate([shared_gate, shared_up, shared_down.T], axis=1)
    packed, after = lax.optimization_barrier((packed, after))
    gathered = lax.all_gather(packed, "dp", axis=0, tiled=True)
    gate_total = jnp.dot(
        normed_rows, gathered[:, :hidden_width], preferred_element_type=jnp.float32
    )
    up_total = jnp.dot(
        normed_rows, gathered[:, hidden_width : 2 * hidden_width], preferred_element_type=jnp.float32
    )
    shared_hidden = (jax.nn.silu(gate_total) * up_total).astype(jnp.bfloat16)
    terms = jnp.einsum(
        "th,dh->td",
        shared_hidden,
        gathered[:, 2 * hidden_width :],
        preferred_element_type=jnp.float32,
    )
    return scatter_sum_mp(terms.astype(jnp.bfloat16))


def on_device(
    tree_query,
    new_kv,
    kv_cache,
    page_table,
    cache_len,
    tree_mask,
    out_weight,
    residual_in,
    norm_gain,
    route_ids,
    route_weight,
    w_gate,
    w_up,
    w_down,
    shared_gate,
    shared_up,
    shared_down,
):
    tok_rows = tree_query.shape[0]
    req_count = cache_len.shape[0]
    tree_len = tree_mask.shape[1]
    head_width = new_kv.shape[2]
    local_heads = tree_query.shape[1] // head_width
    score_scale = head_width ** (-0.5)
    queries = tree_query.reshape(req_count, tree_len, local_heads, head_width)
    queries = queries.transpose(0, 2, 1, 3).reshape(req_count, local_heads * tree_len, head_width)
    tree_keys = new_kv[:, 0, :].reshape(req_count, tree_len, head_width)
    tree_values = new_kv[:, 1, :].reshape(req_count, tree_len, head_width)
    tree_allow = jnp.tile(tree_mask, (1, local_heads, 1)) == 1
    attended = attend_requests(
        queries, tree_keys, tree_values, tree_allow, kv_cache, page_table, cache_len, score_scale
    )
    attended = attended.reshape(req_count, local_heads, tree_len, head_width).transpose(0, 2, 1, 3)
    attended = attended.reshape(tok_rows, local_heads * head_width)
    partial_value = jnp.dot(attended, out_weight, preferred_element_type=jnp.float32)
    model_width = residual_in.shape[1]
    quarter = model_width // lax.axis_size("mp")
    col_start = lax.axis_index("mp") * quarter
    experts = lax.axis_size("dp") * w_gate.shape[0]
    route_count = route_ids.shape[1]
    capacity = min(tok_rows, 4 * tok_rows * route_count // (3 * experts))
    expert_ids = route_ids.reshape(-1)
    onehot = (expert_ids[:, None] == jnp.arange(experts, dtype=jnp.int32)[None, :]).astype(
        jnp.int32
    )
    slot_index = jnp.sum((jnp.cumsum(onehot, axis=0) - onehot) * onehot, axis=1)
    own_residual = lax.dynamic_slice_in_dim(residual_in, col_start, quarter, 1)
    own_stream = (own_residual.astype(jnp.float32) + scatter_sum_mp(partial_value)).astype(jnp.bfloat16)
    stream = gather_mp(own_stream, 1)
    normed_rows = normalize(stream, norm_gain)
    codes = (expert_ids * capacity + slot_index).reshape(tok_rows, route_count)
    slots = jnp.arange(experts * capacity, dtype=jnp.int32)
    placing = jnp.any(codes[None, :, :] == slots[:, None, None], axis=2).astype(jnp.bfloat16)
    own_normed = lax.dynamic_slice_in_dim(normed_rows, col_start, quarter, 1)
    buffer = jnp.dot(placing, own_normed, preferred_element_type=jnp.float32).astype(jnp.bfloat16)
    buffer = buffer.reshape(experts, capacity, quarter)
    received = lax.all_to_all(buffer, "dp", split_axis=0, concat_axis=0, tiled=True)
    results = run_experts(
        gather_mp(received.reshape(experts * capacity, quarter), 1).reshape(
            experts, capacity, model_width
        ),
        w_gate,
        w_up,
        w_down,
    )
    shared_out = shared_experts(normed_rows, shared_gate, shared_up, shared_down, received)
    result_rows = results.reshape(experts * capacity, quarter)
    picked = (
        result_rows[expert_ids * capacity + slot_index]
        .reshape(tok_rows, route_count, quarter)
        .astype(jnp.float32)
    )
    mixture = jnp.einsum("tk,tkc->tc", route_weight, picked, precision=lax.Precision.HIGHEST)
    return (own_stream.astype(jnp.float32) + shared_out.astype(jnp.float32) + mixture).astype(
        jnp.bfloat16
    )


def solution(mesh):
    return jax.shard_map(
        on_device,
        mesh=mesh,
        in_specs=(
            P("dp", "mp"),
            P("dp", None, "mp"),
            P("dp", None, None, "mp"),
            P("dp", None),
            P("dp"),
            P("dp", None, None),
            P("mp", None),
            P("dp", None),
            P(),
            P("dp", None),
            P("dp", None),
            P("dp", None, "mp"),
            P("dp", None, "mp"),
            P("dp", None, "mp"),
            P("dp", "mp"),
            P("dp", "mp"),
            P("mp", "dp"),
        ),
        out_specs=P("dp", "mp"),
        check_vma=False,
    )
```

```python
import jax
import jax.numpy as jnp
from jax import lax
from jax.sharding import PartitionSpec as P

NEGATIVE_FILL = -1e30
DP = ("dpo", "core")
EPSILON = 1e-05


def normalize(rows, gain):
    values = rows.astype(jnp.float32)
    mean_square = jnp.mean(values * values, axis=-1, keepdims=True)
    return (values * lax.rsqrt(mean_square + EPSILON) * gain).astype(jnp.bfloat16)


def attend_requests(
    queries, tree_keys, tree_values, tree_allow, kv_cache, page_table, cache_len, score_scale
):
    pool_pages, _, page_rows, head_width = kv_cache.shape
    pool_keys = kv_cache[:, 0].reshape(pool_pages * page_rows, head_width)
    pool_values = kv_cache[:, 1].reshape(pool_pages * page_rows, head_width)
    page_start = jnp.arange(page_table.shape[1], dtype=jnp.int32) * page_rows
    rows_left = cache_len[:, None] - page_start[None, :]
    live_rows = jnp.where(rows_left > 0, jnp.minimum(rows_left, page_rows), 0)
    slot_ids = jnp.arange(pool_pages, dtype=jnp.int32)
    owns = page_table[:, :, None] == slot_ids[None, None, :]
    slot_rows = jnp.sum(jnp.where(owns, live_rows[:, :, None], 0), axis=1)
    row_ids = jnp.arange(page_rows, dtype=jnp.int32)
    live_mask = (row_ids[None, None, :] < slot_rows[:, :, None]).reshape(
        cache_len.shape[0], 1, pool_pages * page_rows
    )
    cache_scores = (
        jnp.einsum("rqd,kd->rqk", queries, pool_keys, preferred_element_type=jnp.float32)
        * score_scale
    )
    cache_scores = jnp.where(live_mask, cache_scores, NEGATIVE_FILL)
    tree_scores = (
        jnp.einsum("rqd,rud->rqu", queries, tree_keys, preferred_element_type=jnp.float32)
        * score_scale
    )
    tree_scores = jnp.where(tree_allow, tree_scores, NEGATIVE_FILL)
    row_peak = jnp.maximum(jnp.max(cache_scores, axis=2), jnp.max(tree_scores, axis=2))[..., None]
    cache_probs = jnp.where(live_mask, jnp.exp(cache_scores - row_peak), 0.0)
    tree_probs = jnp.where(tree_allow, jnp.exp(tree_scores - row_peak), 0.0)
    denom_sum = jnp.sum(cache_probs, axis=2) + jnp.sum(tree_probs, axis=2)
    weighted = jnp.einsum(
        "rqk,kd->rqd", cache_probs.astype(jnp.bfloat16), pool_values,
        preferred_element_type=jnp.float32,
    )
    weighted = weighted + jnp.einsum(
        "rqu,rud->rqd", tree_probs.astype(jnp.bfloat16), tree_values,
        preferred_element_type=jnp.float32,
    )
    return (weighted / denom_sum[..., None]).astype(jnp.bfloat16)


def gather_mp(block, axis):
    parts = lax.axis_size("mp")
    copies = jnp.broadcast_to(block[None], (parts,) + block.shape)
    pieces = lax.all_to_all(copies, "mp", split_axis=0, concat_axis=0, tiled=True)
    pieces = jnp.moveaxis(pieces, 0, axis)
    shape = list(block.shape)
    shape[axis] = shape[axis] * parts
    return pieces.reshape(shape)


def scatter_sum_mp(terms):
    parts = lax.axis_size("mp")
    rows, width = terms.shape
    blocks = terms.reshape(rows, parts, width // parts).transpose(1, 0, 2)
    pieces = lax.all_to_all(blocks, "mp", split_axis=0, concat_axis=0, tiled=True)
    return jnp.sum(pieces.astype(jnp.float32), axis=0)


def exchange_dp(blocks):
    cores = lax.axis_size("core")
    chips = lax.axis_size("dpo")
    rest = blocks.shape[1:]
    split = blocks.reshape((chips, cores) + rest)
    split = lax.all_to_all(split, "core", split_axis=1, concat_axis=1, tiled=True)
    split = lax.all_to_all(split, "dpo", split_axis=0, concat_axis=0, tiled=True)
    return split.reshape(blocks.shape)


def run_experts(rows, w_gate, w_up, w_down):
    source_count, slot_count, model_width = rows.shape
    flat_rows = rows.reshape(source_count * slot_count, model_width)
    gate_proj = jnp.dot(flat_rows, w_gate[0], preferred_element_type=jnp.float32)
    up_proj = jnp.dot(flat_rows, w_up[0], preferred_element_type=jnp.float32)
    hidden_act = (jax.nn.silu(gate_proj) * up_proj).astype(jnp.bfloat16)
    down_rows = w_down[0]
    summed = jnp.dot(
        gather_mp(hidden_act, 1),
        down_rows,
        preferred_element_type=jnp.float32,
    )
    outputs = summed.astype(jnp.bfloat16).reshape(source_count, slot_count, w_down.shape[2])
    return exchange_dp(outputs)


def shared_experts(normed_rows, shared_gate, shared_up, shared_down, after):
    hidden_width = shared_gate.shape[1]
    packed = jnp.concatenate([shared_gate, shared_up, shared_down.T], axis=1)
    packed, after = lax.optimization_barrier((packed, after))
    gathered = lax.all_gather(packed, DP, axis=0, tiled=True)
    gate_total = jnp.dot(
        normed_rows, gathered[:, :hidden_width], preferred_element_type=jnp.float32
    )
    up_total = jnp.dot(
        normed_rows, gathered[:, hidden_width : 2 * hidden_width], preferred_element_type=jnp.float32
    )
    shared_hidden = (jax.nn.silu(gate_total) * up_total).astype(jnp.bfloat16)
    terms = jnp.einsum(
        "th,dh->td",
        shared_hidden,
        gathered[:, 2 * hidden_width :],
        preferred_element_type=jnp.float32,
    )
    return scatter_sum_mp(terms.astype(jnp.bfloat16))


def on_device(
    tree_query,
    new_kv,
    kv_cache,
    page_table,
    cache_len,
    tree_mask,
    out_weight,
    residual_in,
    norm_gain,
    route_ids,
    route_weight,
    w_gate,
    w_up,
    w_down,
    shared_gate,
    shared_up,
    shared_down,
):
    tok_rows = tree_query.shape[0]
    req_count = cache_len.shape[0]
    tree_len = tree_mask.shape[1]
    head_width = new_kv.shape[2]
    local_heads = tree_query.shape[1] // head_width
    score_scale = head_width ** (-0.5)
    queries = tree_query.reshape(req_count, tree_len, local_heads, head_width)
    queries = queries.transpose(0, 2, 1, 3).reshape(req_count, local_heads * tree_len, head_width)
    tree_keys = new_kv[:, 0, :].reshape(req_count, tree_len, head_width)
    tree_values = new_kv[:, 1, :].reshape(req_count, tree_len, head_width)
    tree_allow = jnp.tile(tree_mask, (1, local_heads, 1)) == 1
    attended = attend_requests(
        queries, tree_keys, tree_values, tree_allow, kv_cache, page_table, cache_len, score_scale
    )
    attended = attended.reshape(req_count, local_heads, tree_len, head_width).transpose(0, 2, 1, 3)
    attended = attended.reshape(tok_rows, local_heads * head_width)
    partial_value = jnp.dot(attended, out_weight, preferred_element_type=jnp.float32)
    model_width = residual_in.shape[1]
    quarter = model_width // lax.axis_size("mp")
    col_start = lax.axis_index("mp") * quarter
    experts = lax.axis_size(DP) * w_gate.shape[0]
    route_count = route_ids.shape[1]
    capacity = min(tok_rows, 4 * tok_rows * route_count // (3 * experts))
    expert_ids = route_ids.reshape(-1)
    onehot = (expert_ids[:, None] == jnp.arange(experts, dtype=jnp.int32)[None, :]).astype(
        jnp.int32
    )
    slot_index = jnp.sum((jnp.cumsum(onehot, axis=0) - onehot) * onehot, axis=1)
    own_residual = lax.dynamic_slice_in_dim(residual_in, col_start, quarter, 1)
    own_stream = (own_residual.astype(jnp.float32) + scatter_sum_mp(partial_value)).astype(jnp.bfloat16)
    stream = gather_mp(own_stream, 1)
    normed_rows = normalize(stream, norm_gain)
    codes = (expert_ids * capacity + slot_index).reshape(tok_rows, route_count)
    slots = jnp.arange(experts * capacity, dtype=jnp.int32)
    placing = jnp.any(codes[None, :, :] == slots[:, None, None], axis=2).astype(jnp.bfloat16)
    own_normed = lax.dynamic_slice_in_dim(normed_rows, col_start, quarter, 1)
    buffer = jnp.dot(placing, own_normed, preferred_element_type=jnp.float32).astype(jnp.bfloat16)
    buffer = buffer.reshape(experts, capacity, quarter)
    received = exchange_dp(buffer)
    results = run_experts(
        gather_mp(received.reshape(experts * capacity, quarter), 1).reshape(
            experts, capacity, model_width
        ),
        w_gate,
        w_up,
        w_down,
    )
    shared_out = shared_experts(normed_rows, shared_gate, shared_up, shared_down, received)
    result_rows = results.reshape(experts * capacity, quarter)
    picked = (
        result_rows[expert_ids * capacity + slot_index]
        .reshape(tok_rows, route_count, quarter)
        .astype(jnp.float32)
    )
    mixture = jnp.einsum("tk,tkc->tc", route_weight, picked, precision=lax.Precision.HIGHEST)
    return (own_stream.astype(jnp.float32) + shared_out.astype(jnp.float32) + mixture).astype(
        jnp.bfloat16
    )


def solution(mesh):
    dp_size, mp_size = mesh.devices.shape
    split_mesh = jax.sharding.Mesh(
        mesh.devices.reshape(dp_size // 2, 2, mp_size), ("dpo", "core", "mp")
    )
    return jax.shard_map(
        on_device,
        mesh=split_mesh,
        in_specs=(
            P(DP, "mp"),
            P(DP, None, "mp"),
            P(DP, None, None, "mp"),
            P(DP, None),
            P(DP),
            P(DP, None, None),
            P("mp", None),
            P(DP, None),
            P(),
            P(DP, None),
            P(DP, None),
            P(DP, None, "mp"),
            P(DP, None, "mp"),
            P(DP, None, "mp"),
            P(DP, "mp"),
            P(DP, "mp"),
            P("mp", DP),
        ),
        out_specs=P(DP, "mp"),
        check_vma=False,
    )
```

```python
import jax
import jax.numpy as jnp
from jax import lax
from jax.sharding import PartitionSpec as P

NEGATIVE_FILL = -1e30
EPSILON = 1e-05


def normalize(rows, gain):
    values = rows.astype(jnp.float32)
    mean_square = jnp.mean(values * values, axis=-1, keepdims=True)
    return (values * lax.rsqrt(mean_square + EPSILON) * gain).astype(jnp.bfloat16)


def attend_requests(
    queries, tree_keys, tree_values, tree_allow, kv_cache, page_table, cache_len, score_scale
):
    pool_pages, _, page_rows, head_width = kv_cache.shape
    pool_keys = kv_cache[:, 0].reshape(pool_pages * page_rows, head_width)
    pool_values = kv_cache[:, 1].reshape(pool_pages * page_rows, head_width)
    page_start = jnp.arange(page_table.shape[1], dtype=jnp.int32) * page_rows
    rows_left = cache_len[:, None] - page_start[None, :]
    live_rows = jnp.where(rows_left > 0, jnp.minimum(rows_left, page_rows), 0)
    slot_ids = jnp.arange(pool_pages, dtype=jnp.int32)
    owns = page_table[:, :, None] == slot_ids[None, None, :]
    slot_rows = jnp.sum(jnp.where(owns, live_rows[:, :, None], 0), axis=1)
    row_ids = jnp.arange(page_rows, dtype=jnp.int32)
    live_mask = (row_ids[None, None, :] < slot_rows[:, :, None]).reshape(
        cache_len.shape[0], 1, pool_pages * page_rows
    )
    cache_scores = (
        jnp.einsum("rqd,kd->rqk", queries, pool_keys, preferred_element_type=jnp.float32)
        * score_scale
    )
    cache_scores = jnp.where(live_mask, cache_scores, NEGATIVE_FILL)
    tree_scores = (
        jnp.einsum("rqd,rud->rqu", queries, tree_keys, preferred_element_type=jnp.float32)
        * score_scale
    )
    tree_scores = jnp.where(tree_allow, tree_scores, NEGATIVE_FILL)
    row_peak = jnp.maximum(jnp.max(cache_scores, axis=2), jnp.max(tree_scores, axis=2))[..., None]
    cache_probs = jnp.where(live_mask, jnp.exp(cache_scores - row_peak), 0.0)
    tree_probs = jnp.where(tree_allow, jnp.exp(tree_scores - row_peak), 0.0)
    denom_sum = jnp.sum(cache_probs, axis=2) + jnp.sum(tree_probs, axis=2)
    weighted = jnp.einsum(
        "rqk,kd->rqd", cache_probs.astype(jnp.bfloat16), pool_values,
        preferred_element_type=jnp.float32,
    )
    weighted = weighted + jnp.einsum(
        "rqu,rud->rqd", tree_probs.astype(jnp.bfloat16), tree_values,
        preferred_element_type=jnp.float32,
    )
    return (weighted / denom_sum[..., None]).astype(jnp.bfloat16)


def gather_mp(block, axis):
    parts = lax.axis_size("mp")
    copies = jnp.broadcast_to(block[None], (parts,) + block.shape)
    pieces = lax.all_to_all(copies, "mp", split_axis=0, concat_axis=0, tiled=True)
    pieces = jnp.moveaxis(pieces, 0, axis)
    shape = list(block.shape)
    shape[axis] = shape[axis] * parts
    return pieces.reshape(shape)


def ring_gather_mp(block):
    parts = lax.axis_size("mp")
    rows, width = block.shape
    half = rows // 2
    to_right = [(k, (k + 1) % parts) for k in range(parts)]
    to_left = [(k, (k - 1) % parts) for k in range(parts)]
    from_left = lax.ppermute(block, "mp", to_right)
    from_right = lax.ppermute(block, "mp", to_left)
    far_top = lax.ppermute(from_right[:half], "mp", to_left)
    far_bottom = lax.ppermute(from_left[half:], "mp", to_right)
    far = jnp.concatenate([far_top, far_bottom], axis=0)
    rotated = jnp.concatenate([block, from_right, far, from_left], axis=1)
    return jnp.roll(rotated, lax.axis_index("mp") * width, axis=1)


def scatter_sum_mp(terms):
    parts = lax.axis_size("mp")
    rows, width = terms.shape
    blocks = terms.reshape(rows, parts, width // parts).transpose(1, 0, 2)
    pieces = lax.all_to_all(blocks, "mp", split_axis=0, concat_axis=0, tiled=True)
    return jnp.sum(pieces.astype(jnp.float32), axis=0)


def run_experts(rows, w_gate, w_up, w_down):
    source_count, slot_count, model_width = rows.shape
    flat_rows = rows.reshape(source_count * slot_count, model_width)
    gate_proj = jnp.dot(flat_rows, w_gate[0], preferred_element_type=jnp.float32)
    up_proj = jnp.dot(flat_rows, w_up[0], preferred_element_type=jnp.float32)
    hidden_act = (jax.nn.silu(gate_proj) * up_proj).astype(jnp.bfloat16)
    down_rows = w_down[0]
    summed = jnp.dot(
        ring_gather_mp(hidden_act),
        down_rows,
        preferred_element_type=jnp.float32,
    )
    outputs = summed.astype(jnp.bfloat16).reshape(source_count, slot_count, w_down.shape[2])
    return lax.all_to_all(outputs, "dp", split_axis=0, concat_axis=0, tiled=True)


def shared_experts(normed_rows, shared_gate, shared_up, shared_down, after):
    hidden_width = shared_gate.shape[1]
    packed = jnp.concatenate([shared_gate, shared_up, shared_down.T], axis=1)
    packed, after = lax.optimization_barrier((packed, after))
    gathered = lax.all_gather(packed, "dp", axis=0, tiled=True)
    gate_total = jnp.dot(
        normed_rows, gathered[:, :hidden_width], preferred_element_type=jnp.float32
    )
    up_total = jnp.dot(
        normed_rows, gathered[:, hidden_width : 2 * hidden_width], preferred_element_type=jnp.float32
    )
    shared_hidden = (jax.nn.silu(gate_total) * up_total).astype(jnp.bfloat16)
    terms = jnp.einsum(
        "th,dh->td",
        shared_hidden,
        gathered[:, 2 * hidden_width :],
        preferred_element_type=jnp.float32,
    )
    return scatter_sum_mp(terms.astype(jnp.bfloat16))


def on_device(
    tree_query,
    new_kv,
    kv_cache,
    page_table,
    cache_len,
    tree_mask,
    out_weight,
    residual_in,
    norm_gain,
    route_ids,
    route_weight,
    w_gate,
    w_up,
    w_down,
    shared_gate,
    shared_up,
    shared_down,
):
    tok_rows = tree_query.shape[0]
    req_count = cache_len.shape[0]
    tree_len = tree_mask.shape[1]
    head_width = new_kv.shape[2]
    local_heads = tree_query.shape[1] // head_width
    score_scale = head_width ** (-0.5)
    queries = tree_query.reshape(req_count, tree_len, local_heads, head_width)
    queries = queries.transpose(0, 2, 1, 3).reshape(req_count, local_heads * tree_len, head_width)
    tree_keys = new_kv[:, 0, :].reshape(req_count, tree_len, head_width)
    tree_values = new_kv[:, 1, :].reshape(req_count, tree_len, head_width)
    tree_allow = jnp.tile(tree_mask, (1, local_heads, 1)) == 1
    attended = attend_requests(
        queries, tree_keys, tree_values, tree_allow, kv_cache, page_table, cache_len, score_scale
    )
    attended = attended.reshape(req_count, local_heads, tree_len, head_width).transpose(0, 2, 1, 3)
    attended = attended.reshape(tok_rows, local_heads * head_width)
    partial_value = jnp.dot(attended, out_weight, preferred_element_type=jnp.float32)
    model_width = residual_in.shape[1]
    quarter = model_width // lax.axis_size("mp")
    col_start = lax.axis_index("mp") * quarter
    experts = lax.axis_size("dp") * w_gate.shape[0]
    route_count = route_ids.shape[1]
    capacity = min(tok_rows, 4 * tok_rows * route_count // (3 * experts))
    expert_ids = route_ids.reshape(-1)
    onehot = (expert_ids[:, None] == jnp.arange(experts, dtype=jnp.int32)[None, :]).astype(
        jnp.int32
    )
    slot_index = jnp.sum((jnp.cumsum(onehot, axis=0) - onehot) * onehot, axis=1)
    own_residual = lax.dynamic_slice_in_dim(residual_in, col_start, quarter, 1)
    own_stream = (own_residual.astype(jnp.float32) + scatter_sum_mp(partial_value)).astype(jnp.bfloat16)
    stream = gather_mp(own_stream, 1)
    normed_rows = normalize(stream, norm_gain)
    codes = (expert_ids * capacity + slot_index).reshape(tok_rows, route_count)
    slots = jnp.arange(experts * capacity, dtype=jnp.int32)
    placing = jnp.any(codes[None, :, :] == slots[:, None, None], axis=2).astype(jnp.bfloat16)
    own_normed = lax.dynamic_slice_in_dim(normed_rows, col_start, quarter, 1)
    buffer = jnp.dot(placing, own_normed, preferred_element_type=jnp.float32).astype(jnp.bfloat16)
    buffer = buffer.reshape(experts, capacity, quarter)
    received = lax.all_to_all(buffer, "dp", split_axis=0, concat_axis=0, tiled=True)
    results = run_experts(
        ring_gather_mp(received.reshape(experts * capacity, quarter)).reshape(
            experts, capacity, model_width
        ),
        w_gate,
        w_up,
        w_down,
    )
    shared_out = shared_experts(normed_rows, shared_gate, shared_up, shared_down, received)
    result_rows = results.reshape(experts * capacity, quarter)
    picked = (
        result_rows[expert_ids * capacity + slot_index]
        .reshape(tok_rows, route_count, quarter)
        .astype(jnp.float32)
    )
    mixture = jnp.einsum("tk,tkc->tc", route_weight, picked, precision=lax.Precision.HIGHEST)
    return (own_stream.astype(jnp.float32) + shared_out.astype(jnp.float32) + mixture).astype(
        jnp.bfloat16
    )


def solution(mesh):
    return jax.shard_map(
        on_device,
        mesh=mesh,
        in_specs=(
            P("dp", "mp"),
            P("dp", None, "mp"),
            P("dp", None, None, "mp"),
            P("dp", None),
            P("dp"),
            P("dp", None, None),
            P("mp", None),
            P("dp", None),
            P(),
            P("dp", None),
            P("dp", None),
            P("dp", None, "mp"),
            P("dp", None, "mp"),
            P("dp", None, "mp"),
            P("dp", "mp"),
            P("dp", "mp"),
            P("mp", "dp"),
        ),
        out_specs=P("dp", "mp"),
        check_vma=False,
    )
```

```python
import jax
import jax.numpy as jnp
from jax import lax
from jax.sharding import PartitionSpec as P

NEGATIVE_FILL = -1e30
EPSILON = 1e-05


def normalize(rows, gain):
    values = rows.astype(jnp.float32)
    mean_square = jnp.mean(values * values, axis=-1, keepdims=True)
    return (values * lax.rsqrt(mean_square + EPSILON) * gain).astype(jnp.bfloat16)


def attend_requests(
    queries, tree_keys, tree_values, tree_allow, kv_cache, page_table, cache_len, score_scale
):
    pool_pages, _, page_rows, head_width = kv_cache.shape
    pool_keys = kv_cache[:, 0].reshape(pool_pages * page_rows, head_width)
    pool_values = kv_cache[:, 1].reshape(pool_pages * page_rows, head_width)
    page_start = jnp.arange(page_table.shape[1], dtype=jnp.int32) * page_rows
    rows_left = cache_len[:, None] - page_start[None, :]
    live_rows = jnp.where(rows_left > 0, jnp.minimum(rows_left, page_rows), 0)
    slot_ids = jnp.arange(pool_pages, dtype=jnp.int32)
    owns = page_table[:, :, None] == slot_ids[None, None, :]
    slot_rows = jnp.sum(jnp.where(owns, live_rows[:, :, None], 0), axis=1)
    row_ids = jnp.arange(page_rows, dtype=jnp.int32)
    live_mask = (row_ids[None, None, :] < slot_rows[:, :, None]).reshape(
        cache_len.shape[0], 1, pool_pages * page_rows
    )
    cache_scores = (
        jnp.einsum("rqd,kd->rqk", queries, pool_keys, preferred_element_type=jnp.float32)
        * score_scale
    )
    cache_scores = jnp.where(live_mask, cache_scores, NEGATIVE_FILL)
    tree_scores = (
        jnp.einsum("rqd,rud->rqu", queries, tree_keys, preferred_element_type=jnp.float32)
        * score_scale
    )
    tree_scores = jnp.where(tree_allow, tree_scores, NEGATIVE_FILL)
    row_peak = jnp.maximum(jnp.max(cache_scores, axis=2), jnp.max(tree_scores, axis=2))[..., None]
    cache_probs = jnp.where(live_mask, jnp.exp(cache_scores - row_peak), 0.0)
    tree_probs = jnp.where(tree_allow, jnp.exp(tree_scores - row_peak), 0.0)
    denom_sum = jnp.sum(cache_probs, axis=2) + jnp.sum(tree_probs, axis=2)
    weighted = jnp.einsum(
        "rqk,kd->rqd", cache_probs.astype(jnp.bfloat16), pool_values,
        preferred_element_type=jnp.float32,
    )
    weighted = weighted + jnp.einsum(
        "rqu,rud->rqd", tree_probs.astype(jnp.bfloat16), tree_values,
        preferred_element_type=jnp.float32,
    )
    return (weighted / denom_sum[..., None]).astype(jnp.bfloat16)


def gather_mp(block, axis):
    parts = lax.axis_size("mp")
    copies = jnp.broadcast_to(block[None], (parts,) + block.shape)
    pieces = lax.all_to_all(copies, "mp", split_axis=0, concat_axis=0, tiled=True)
    pieces = jnp.moveaxis(pieces, 0, axis)
    shape = list(block.shape)
    shape[axis] = shape[axis] * parts
    return pieces.reshape(shape)


def ring_blocks_mp(block):
    parts = lax.axis_size("mp")
    half = block.shape[0] // 2
    to_right = [(k, (k + 1) % parts) for k in range(parts)]
    to_left = [(k, (k - 1) % parts) for k in range(parts)]
    from_left = lax.ppermute(block, "mp", to_right)
    from_right = lax.ppermute(block, "mp", to_left)
    far_top = lax.ppermute(from_right[:half], "mp", to_left)
    far_bottom = lax.ppermute(from_left[half:], "mp", to_right)
    far = jnp.concatenate([far_top, far_bottom], axis=0)
    return [block, from_right, far, from_left]


def blockwise_dot(blocks, weights):
    parts = lax.axis_size("mp")
    mp_index = lax.axis_index("mp")
    width = blocks[0].shape[1]
    total = None
    for step, piece in enumerate(blocks):
        start = ((mp_index + step) % parts) * width
        rows = lax.dynamic_slice_in_dim(weights, start, width, 0)
        term = jnp.dot(piece, rows, preferred_element_type=jnp.float32)
        total = term if total is None else total + term
    return total


def scatter_sum_mp(terms):
    parts = lax.axis_size("mp")
    rows, width = terms.shape
    blocks = terms.reshape(rows, parts, width // parts).transpose(1, 0, 2)
    pieces = lax.all_to_all(blocks, "mp", split_axis=0, concat_axis=0, tiled=True)
    return jnp.sum(pieces.astype(jnp.float32), axis=0)


def run_experts(row_blocks, source_count, slot_count, w_gate, w_up, w_down):
    gate_proj = blockwise_dot(row_blocks, w_gate[0])
    up_proj = blockwise_dot(row_blocks, w_up[0])
    hidden_act = (jax.nn.silu(gate_proj) * up_proj).astype(jnp.bfloat16)
    summed = blockwise_dot(ring_blocks_mp(hidden_act), w_down[0])
    outputs = summed.astype(jnp.bfloat16).reshape(source_count, slot_count, w_down.shape[2])
    return lax.all_to_all(outputs, "dp", split_axis=0, concat_axis=0, tiled=True)


def shared_experts(normed_rows, shared_gate, shared_up, shared_down, after):
    hidden_width = shared_gate.shape[1]
    packed = jnp.concatenate([shared_gate, shared_up, shared_down.T], axis=1)
    packed, after = lax.optimization_barrier((packed, after))
    gathered = lax.all_gather(packed, "dp", axis=0, tiled=True)
    gate_total = jnp.dot(
        normed_rows, gathered[:, :hidden_width], preferred_element_type=jnp.float32
    )
    up_total = jnp.dot(
        normed_rows, gathered[:, hidden_width : 2 * hidden_width], preferred_element_type=jnp.float32
    )
    shared_hidden = (jax.nn.silu(gate_total) * up_total).astype(jnp.bfloat16)
    terms = jnp.einsum(
        "th,dh->td",
        shared_hidden,
        gathered[:, 2 * hidden_width :],
        preferred_element_type=jnp.float32,
    )
    return scatter_sum_mp(terms.astype(jnp.bfloat16))


def on_device(
    tree_query,
    new_kv,
    kv_cache,
    page_table,
    cache_len,
    tree_mask,
    out_weight,
    residual_in,
    norm_gain,
    route_ids,
    route_weight,
    w_gate,
    w_up,
    w_down,
    shared_gate,
    shared_up,
    shared_down,
):
    tok_rows = tree_query.shape[0]
    req_count = cache_len.shape[0]
    tree_len = tree_mask.shape[1]
    head_width = new_kv.shape[2]
    local_heads = tree_query.shape[1] // head_width
    score_scale = head_width ** (-0.5)
    queries = tree_query.reshape(req_count, tree_len, local_heads, head_width)
    queries = queries.transpose(0, 2, 1, 3).reshape(req_count, local_heads * tree_len, head_width)
    tree_keys = new_kv[:, 0, :].reshape(req_count, tree_len, head_width)
    tree_values = new_kv[:, 1, :].reshape(req_count, tree_len, head_width)
    tree_allow = jnp.tile(tree_mask, (1, local_heads, 1)) == 1
    attended = attend_requests(
        queries, tree_keys, tree_values, tree_allow, kv_cache, page_table, cache_len, score_scale
    )
    attended = attended.reshape(req_count, local_heads, tree_len, head_width).transpose(0, 2, 1, 3)
    attended = attended.reshape(tok_rows, local_heads * head_width)
    partial_value = jnp.dot(attended, out_weight, preferred_element_type=jnp.float32)
    model_width = residual_in.shape[1]
    quarter = model_width // lax.axis_size("mp")
    col_start = lax.axis_index("mp") * quarter
    experts = lax.axis_size("dp") * w_gate.shape[0]
    route_count = route_ids.shape[1]
    capacity = min(tok_rows, 4 * tok_rows * route_count // (3 * experts))
    expert_ids = route_ids.reshape(-1)
    onehot = (expert_ids[:, None] == jnp.arange(experts, dtype=jnp.int32)[None, :]).astype(
        jnp.int32
    )
    slot_index = jnp.sum((jnp.cumsum(onehot, axis=0) - onehot) * onehot, axis=1)
    own_residual = lax.dynamic_slice_in_dim(residual_in, col_start, quarter, 1)
    own_stream = (own_residual.astype(jnp.float32) + scatter_sum_mp(partial_value)).astype(jnp.bfloat16)
    stream = gather_mp(own_stream, 1)
    normed_rows = normalize(stream, norm_gain)
    codes = (expert_ids * capacity + slot_index).reshape(tok_rows, route_count)
    slots = jnp.arange(experts * capacity, dtype=jnp.int32)
    placing = jnp.any(codes[None, :, :] == slots[:, None, None], axis=2).astype(jnp.bfloat16)
    own_normed = lax.dynamic_slice_in_dim(normed_rows, col_start, quarter, 1)
    buffer = jnp.dot(placing, own_normed, preferred_element_type=jnp.float32).astype(jnp.bfloat16)
    buffer = buffer.reshape(experts, capacity, quarter)
    received = lax.all_to_all(buffer, "dp", split_axis=0, concat_axis=0, tiled=True)
    results = run_experts(
        ring_blocks_mp(received.reshape(experts * capacity, quarter)),
        experts,
        capacity,
        w_gate,
        w_up,
        w_down,
    )
    shared_out = shared_experts(normed_rows, shared_gate, shared_up, shared_down, received)
    result_rows = results.reshape(experts * capacity, quarter)
    picked = (
        result_rows[expert_ids * capacity + slot_index]
        .reshape(tok_rows, route_count, quarter)
        .astype(jnp.float32)
    )
    mixture = jnp.einsum("tk,tkc->tc", route_weight, picked, precision=lax.Precision.HIGHEST)
    return (own_stream.astype(jnp.float32) + shared_out.astype(jnp.float32) + mixture).astype(
        jnp.bfloat16
    )


def solution(mesh):
    return jax.shard_map(
        on_device,
        mesh=mesh,
        in_specs=(
            P("dp", "mp"),
            P("dp", None, "mp"),
            P("dp", None, None, "mp"),
            P("dp", None),
            P("dp"),
            P("dp", None, None),
            P("mp", None),
            P("dp", None),
            P(),
            P("dp", None),
            P("dp", None),
            P("dp", None, "mp"),
            P("dp", None, "mp"),
            P("dp", None, "mp"),
            P("dp", "mp"),
            P("dp", "mp"),
            P("mp", "dp"),
        ),
        out_specs=P("dp", "mp"),
        check_vma=False,
    )
```

```python
import jax
import jax.numpy as jnp
from jax import lax
from jax.sharding import PartitionSpec as P

NEGATIVE_FILL = -1e30
EPSILON = 1e-05


def normalize(rows, gain):
    values = rows.astype(jnp.float32)
    mean_square = jnp.mean(values * values, axis=-1, keepdims=True)
    return (values * lax.rsqrt(mean_square + EPSILON) * gain).astype(jnp.bfloat16)


def attend_requests(
    queries, tree_keys, tree_values, tree_allow, kv_cache, page_table, cache_len, score_scale
):
    pool_pages, _, page_rows, head_width = kv_cache.shape
    pool_keys = kv_cache[:, 0].reshape(pool_pages * page_rows, head_width)
    pool_values = kv_cache[:, 1].reshape(pool_pages * page_rows, head_width)
    page_start = jnp.arange(page_table.shape[1], dtype=jnp.int32) * page_rows
    rows_left = cache_len[:, None] - page_start[None, :]
    live_rows = jnp.where(rows_left > 0, jnp.minimum(rows_left, page_rows), 0)
    slot_ids = jnp.arange(pool_pages, dtype=jnp.int32)
    owns = page_table[:, :, None] == slot_ids[None, None, :]
    slot_rows = jnp.sum(jnp.where(owns, live_rows[:, :, None], 0), axis=1)
    row_ids = jnp.arange(page_rows, dtype=jnp.int32)
    live_mask = (row_ids[None, None, :] < slot_rows[:, :, None]).reshape(
        cache_len.shape[0], 1, pool_pages * page_rows
    )
    cache_scores = (
        jnp.einsum("rqd,kd->rqk", queries, pool_keys, preferred_element_type=jnp.float32)
        * score_scale
    )
    cache_scores = jnp.where(live_mask, cache_scores, NEGATIVE_FILL)
    tree_scores = (
        jnp.einsum("rqd,rud->rqu", queries, tree_keys, preferred_element_type=jnp.float32)
        * score_scale
    )
    tree_scores = jnp.where(tree_allow, tree_scores, NEGATIVE_FILL)
    row_peak = jnp.maximum(jnp.max(cache_scores, axis=2), jnp.max(tree_scores, axis=2))[..., None]
    cache_probs = jnp.where(live_mask, jnp.exp(cache_scores - row_peak), 0.0)
    tree_probs = jnp.where(tree_allow, jnp.exp(tree_scores - row_peak), 0.0)
    denom_sum = jnp.sum(cache_probs, axis=2) + jnp.sum(tree_probs, axis=2)
    weighted = jnp.einsum(
        "rqk,kd->rqd", cache_probs.astype(jnp.bfloat16), pool_values,
        preferred_element_type=jnp.float32,
    )
    weighted = weighted + jnp.einsum(
        "rqu,rud->rqd", tree_probs.astype(jnp.bfloat16), tree_values,
        preferred_element_type=jnp.float32,
    )
    return (weighted / denom_sum[..., None]).astype(jnp.bfloat16)


def gather_mp(block, axis):
    parts = lax.axis_size("mp")
    copies = jnp.broadcast_to(block[None], (parts,) + block.shape)
    pieces = lax.all_to_all(copies, "mp", split_axis=0, concat_axis=0, tiled=True)
    pieces = jnp.moveaxis(pieces, 0, axis)
    shape = list(block.shape)
    shape[axis] = shape[axis] * parts
    return pieces.reshape(shape)


def ring_blocks_mp(block):
    parts = lax.axis_size("mp")
    half = block.shape[0] // 2
    to_right = [(k, (k + 1) % parts) for k in range(parts)]
    to_left = [(k, (k - 1) % parts) for k in range(parts)]
    from_left = lax.ppermute(block, "mp", to_right)
    from_right = lax.ppermute(block, "mp", to_left)
    far_top = lax.ppermute(from_right[:half], "mp", to_left)
    far_bottom = lax.ppermute(from_left[half:], "mp", to_right)
    far = jnp.concatenate([far_top, far_bottom], axis=0)
    return [block, from_right, far, from_left]


def blockwise_dot(blocks, weights):
    parts = lax.axis_size("mp")
    mp_index = lax.axis_index("mp")
    width = blocks[0].shape[1]
    total = None
    for step, piece in enumerate(blocks):
        start = ((mp_index + step) % parts) * width
        rows = lax.dynamic_slice_in_dim(weights, start, width, 0)
        term = jnp.dot(piece, rows, preferred_element_type=jnp.float32)
        total = term if total is None else total + term
    return total


def scatter_sum_mp(terms):
    parts = lax.axis_size("mp")
    rows, width = terms.shape
    blocks = terms.reshape(rows, parts, width // parts).transpose(1, 0, 2)
    pieces = lax.all_to_all(blocks, "mp", split_axis=0, concat_axis=0, tiled=True)
    return jnp.sum(pieces.astype(jnp.float32), axis=0)


def run_experts(row_blocks, source_count, slot_count, w_gate, w_up, w_down):
    gate_proj = blockwise_dot(row_blocks, w_gate[0])
    up_proj = blockwise_dot(row_blocks, w_up[0])
    hidden_act = (jax.nn.silu(gate_proj) * up_proj).astype(jnp.bfloat16)
    summed = blockwise_dot(ring_blocks_mp(hidden_act), w_down[0])
    outputs = summed.astype(jnp.bfloat16).reshape(source_count, slot_count, w_down.shape[2])
    return lax.all_to_all(outputs, "dp", split_axis=0, concat_axis=0, tiled=True)


def shared_experts(normed_rows, shared_gate, shared_up, shared_down, after):
    hidden_width = shared_gate.shape[1]
    packed = jnp.concatenate([shared_gate, shared_up, shared_down.T], axis=1)
    packed, after = lax.optimization_barrier((packed, after))
    gathered = lax.all_gather(packed, "dp", axis=0, tiled=True)
    gate_total = jnp.dot(
        normed_rows, gathered[:, :hidden_width], preferred_element_type=jnp.float32
    )
    up_total = jnp.dot(
        normed_rows, gathered[:, hidden_width : 2 * hidden_width], preferred_element_type=jnp.float32
    )
    shared_hidden = (jax.nn.silu(gate_total) * up_total).astype(jnp.bfloat16)
    terms = jnp.einsum(
        "th,dh->td",
        shared_hidden,
        gathered[:, 2 * hidden_width :],
        preferred_element_type=jnp.float32,
    )
    return lax.psum_scatter(terms.astype(jnp.bfloat16), "mp", scatter_dimension=1, tiled=True)


def on_device(
    tree_query,
    new_kv,
    kv_cache,
    page_table,
    cache_len,
    tree_mask,
    out_weight,
    residual_in,
    norm_gain,
    route_ids,
    route_weight,
    w_gate,
    w_up,
    w_down,
    shared_gate,
    shared_up,
    shared_down,
):
    tok_rows = tree_query.shape[0]
    req_count = cache_len.shape[0]
    tree_len = tree_mask.shape[1]
    head_width = new_kv.shape[2]
    local_heads = tree_query.shape[1] // head_width
    score_scale = head_width ** (-0.5)
    queries = tree_query.reshape(req_count, tree_len, local_heads, head_width)
    queries = queries.transpose(0, 2, 1, 3).reshape(req_count, local_heads * tree_len, head_width)
    tree_keys = new_kv[:, 0, :].reshape(req_count, tree_len, head_width)
    tree_values = new_kv[:, 1, :].reshape(req_count, tree_len, head_width)
    tree_allow = jnp.tile(tree_mask, (1, local_heads, 1)) == 1
    attended = attend_requests(
        queries, tree_keys, tree_values, tree_allow, kv_cache, page_table, cache_len, score_scale
    )
    attended = attended.reshape(req_count, local_heads, tree_len, head_width).transpose(0, 2, 1, 3)
    attended = attended.reshape(tok_rows, local_heads * head_width)
    partial_value = jnp.dot(attended, out_weight, preferred_element_type=jnp.float32)
    model_width = residual_in.shape[1]
    quarter = model_width // lax.axis_size("mp")
    col_start = lax.axis_index("mp") * quarter
    experts = lax.axis_size("dp") * w_gate.shape[0]
    route_count = route_ids.shape[1]
    capacity = min(tok_rows, 4 * tok_rows * route_count // (3 * experts))
    expert_ids = route_ids.reshape(-1)
    onehot = (expert_ids[:, None] == jnp.arange(experts, dtype=jnp.int32)[None, :]).astype(
        jnp.int32
    )
    slot_index = jnp.sum((jnp.cumsum(onehot, axis=0) - onehot) * onehot, axis=1)
    own_residual = lax.dynamic_slice_in_dim(residual_in, col_start, quarter, 1)
    own_stream = (own_residual.astype(jnp.float32) + scatter_sum_mp(partial_value)).astype(jnp.bfloat16)
    stream = gather_mp(own_stream, 1)
    normed_rows = normalize(stream, norm_gain)
    codes = (expert_ids * capacity + slot_index).reshape(tok_rows, route_count)
    slots = jnp.arange(experts * capacity, dtype=jnp.int32)
    placing = jnp.any(codes[None, :, :] == slots[:, None, None], axis=2).astype(jnp.bfloat16)
    own_normed = lax.dynamic_slice_in_dim(normed_rows, col_start, quarter, 1)
    buffer = jnp.dot(placing, own_normed, preferred_element_type=jnp.float32).astype(jnp.bfloat16)
    buffer = buffer.reshape(experts, capacity, quarter)
    received = lax.all_to_all(buffer, "dp", split_axis=0, concat_axis=0, tiled=True)
    results = run_experts(
        ring_blocks_mp(received.reshape(experts * capacity, quarter)),
        experts,
        capacity,
        w_gate,
        w_up,
        w_down,
    )
    shared_out = shared_experts(normed_rows, shared_gate, shared_up, shared_down, received)
    result_rows = results.reshape(experts * capacity, quarter)
    picked = (
        result_rows[expert_ids * capacity + slot_index]
        .reshape(tok_rows, route_count, quarter)
        .astype(jnp.float32)
    )
    mixture = jnp.einsum("tk,tkc->tc", route_weight, picked, precision=lax.Precision.HIGHEST)
    return (own_stream.astype(jnp.float32) + shared_out.astype(jnp.float32) + mixture).astype(
        jnp.bfloat16
    )


def solution(mesh):
    return jax.shard_map(
        on_device,
        mesh=mesh,
        in_specs=(
            P("dp", "mp"),
            P("dp", None, "mp"),
            P("dp", None, None, "mp"),
            P("dp", None),
            P("dp"),
            P("dp", None, None),
            P("mp", None),
            P("dp", None),
            P(),
            P("dp", None),
            P("dp", None),
            P("dp", None, "mp"),
            P("dp", None, "mp"),
            P("dp", None, "mp"),
            P("dp", "mp"),
            P("dp", "mp"),
            P("mp", "dp"),
        ),
        out_specs=P("dp", "mp"),
        check_vma=False,
    )
```

```python
import jax
import jax.numpy as jnp
from jax import lax
from jax.sharding import PartitionSpec as P

NEGATIVE_FILL = -1e30
EPSILON = 1e-05


def normalize(rows, gain):
    values = rows.astype(jnp.float32)
    mean_square = jnp.mean(values * values, axis=-1, keepdims=True)
    return (values * lax.rsqrt(mean_square + EPSILON) * gain).astype(jnp.bfloat16)


def attend_requests(
    queries, tree_keys, tree_values, tree_allow, kv_cache, page_table, cache_len, score_scale
):
    pool_pages, _, page_rows, head_width = kv_cache.shape
    pool_keys = kv_cache[:, 0].reshape(pool_pages * page_rows, head_width)
    pool_values = kv_cache[:, 1].reshape(pool_pages * page_rows, head_width)
    page_start = jnp.arange(page_table.shape[1], dtype=jnp.int32) * page_rows
    rows_left = cache_len[:, None] - page_start[None, :]
    live_rows = jnp.where(rows_left > 0, jnp.minimum(rows_left, page_rows), 0)
    slot_ids = jnp.arange(pool_pages, dtype=jnp.int32)
    owns = page_table[:, :, None] == slot_ids[None, None, :]
    slot_rows = jnp.sum(jnp.where(owns, live_rows[:, :, None], 0), axis=1)
    row_ids = jnp.arange(page_rows, dtype=jnp.int32)
    live_mask = (row_ids[None, None, :] < slot_rows[:, :, None]).reshape(
        cache_len.shape[0], 1, pool_pages * page_rows
    )
    cache_scores = (
        jnp.einsum("rqd,kd->rqk", queries, pool_keys, preferred_element_type=jnp.float32)
        * score_scale
    )
    cache_scores = jnp.where(live_mask, cache_scores, NEGATIVE_FILL)
    tree_scores = (
        jnp.einsum("rqd,rud->rqu", queries, tree_keys, preferred_element_type=jnp.float32)
        * score_scale
    )
    tree_scores = jnp.where(tree_allow, tree_scores, NEGATIVE_FILL)
    row_peak = jnp.maximum(jnp.max(cache_scores, axis=2), jnp.max(tree_scores, axis=2))[..., None]
    cache_probs = jnp.where(live_mask, jnp.exp(cache_scores - row_peak), 0.0)
    tree_probs = jnp.where(tree_allow, jnp.exp(tree_scores - row_peak), 0.0)
    denom_sum = jnp.sum(cache_probs, axis=2) + jnp.sum(tree_probs, axis=2)
    weighted = jnp.einsum(
        "rqk,kd->rqd", cache_probs.astype(jnp.bfloat16), pool_values,
        preferred_element_type=jnp.float32,
    )
    weighted = weighted + jnp.einsum(
        "rqu,rud->rqd", tree_probs.astype(jnp.bfloat16), tree_values,
        preferred_element_type=jnp.float32,
    )
    return (weighted / denom_sum[..., None]).astype(jnp.bfloat16)


def gather_mp(block, axis):
    parts = lax.axis_size("mp")
    copies = jnp.broadcast_to(block[None], (parts,) + block.shape)
    pieces = lax.all_to_all(copies, "mp", split_axis=0, concat_axis=0, tiled=True)
    pieces = jnp.moveaxis(pieces, 0, axis)
    shape = list(block.shape)
    shape[axis] = shape[axis] * parts
    return pieces.reshape(shape)


def ring_blocks_mp(block):
    parts = lax.axis_size("mp")
    half = block.shape[0] // 2
    to_right = [(k, (k + 1) % parts) for k in range(parts)]
    to_left = [(k, (k - 1) % parts) for k in range(parts)]
    from_left = lax.ppermute(block, "mp", to_right)
    from_right = lax.ppermute(block, "mp", to_left)
    far_top = lax.ppermute(from_right[:half], "mp", to_left)
    far_bottom = lax.ppermute(from_left[half:], "mp", to_right)
    far = jnp.concatenate([far_top, far_bottom], axis=0)
    return [block, from_right, far, from_left]


def blockwise_dot(blocks, weights):
    parts = lax.axis_size("mp")
    mp_index = lax.axis_index("mp")
    width = blocks[0].shape[1]
    total = None
    for step, piece in enumerate(blocks):
        start = ((mp_index + step) % parts) * width
        rows = lax.dynamic_slice_in_dim(weights, start, width, 0)
        term = jnp.dot(piece, rows, preferred_element_type=jnp.float32)
        total = term if total is None else total + term
    return total


def scatter_sum_mp(terms):
    parts = lax.axis_size("mp")
    rows, width = terms.shape
    blocks = terms.reshape(rows, parts, width // parts).transpose(1, 0, 2)
    pieces = lax.all_to_all(blocks, "mp", split_axis=0, concat_axis=0, tiled=True)
    return jnp.sum(pieces.astype(jnp.float32), axis=0)


def run_experts(row_blocks, source_count, slot_count, w_gate, w_up, w_down):
    gate_proj = blockwise_dot(row_blocks, w_gate[0])
    up_proj = blockwise_dot(row_blocks, w_up[0])
    hidden_act = (jax.nn.silu(gate_proj) * up_proj).astype(jnp.bfloat16)
    summed = blockwise_dot(ring_blocks_mp(hidden_act), w_down[0])
    outputs = summed.astype(jnp.bfloat16).reshape(source_count, slot_count, w_down.shape[2])
    return lax.all_to_all(outputs, "dp", split_axis=0, concat_axis=0, tiled=True)


def shared_experts(normed_rows, shared_gate, shared_up, shared_down, after):
    hidden_width = shared_gate.shape[1]
    packed = jnp.concatenate([shared_gate, shared_up, shared_down.T], axis=1)
    packed, after = lax.optimization_barrier((packed, after))
    gathered = lax.all_gather(packed, "dp", axis=0, tiled=True)
    gate_total = jnp.dot(
        normed_rows, gathered[:, :hidden_width], preferred_element_type=jnp.float32
    )
    up_total = jnp.dot(
        normed_rows, gathered[:, hidden_width : 2 * hidden_width], preferred_element_type=jnp.float32
    )
    shared_hidden = (jax.nn.silu(gate_total) * up_total).astype(jnp.bfloat16)
    terms = jnp.einsum(
        "th,dh->td",
        shared_hidden,
        gathered[:, 2 * hidden_width :],
        preferred_element_type=jnp.float32,
    )
    return lax.psum_scatter(terms.astype(jnp.bfloat16), "mp", scatter_dimension=1, tiled=True)


def on_device(
    tree_query,
    new_kv,
    kv_cache,
    page_table,
    cache_len,
    tree_mask,
    out_weight,
    residual_in,
    norm_gain,
    route_ids,
    route_weight,
    w_gate,
    w_up,
    w_down,
    shared_gate,
    shared_up,
    shared_down,
):
    tok_rows = tree_query.shape[0]
    req_count = cache_len.shape[0]
    tree_len = tree_mask.shape[1]
    head_width = new_kv.shape[2]
    local_heads = tree_query.shape[1] // head_width
    score_scale = head_width ** (-0.5)
    queries = tree_query.reshape(req_count, tree_len, local_heads, head_width)
    queries = queries.transpose(0, 2, 1, 3).reshape(req_count, local_heads * tree_len, head_width)
    tree_keys = new_kv[:, 0, :].reshape(req_count, tree_len, head_width)
    tree_values = new_kv[:, 1, :].reshape(req_count, tree_len, head_width)
    tree_allow = jnp.tile(tree_mask, (1, local_heads, 1)) == 1
    attended = attend_requests(
        queries, tree_keys, tree_values, tree_allow, kv_cache, page_table, cache_len, score_scale
    )
    attended = attended.reshape(req_count, local_heads, tree_len, head_width).transpose(0, 2, 1, 3)
    attended = attended.reshape(tok_rows, local_heads * head_width)
    partial_value = jnp.dot(attended, out_weight, preferred_element_type=jnp.float32)
    model_width = residual_in.shape[1]
    quarter = model_width // lax.axis_size("mp")
    col_start = lax.axis_index("mp") * quarter
    experts = lax.axis_size("dp") * w_gate.shape[0]
    route_count = route_ids.shape[1]
    capacity = min(tok_rows, 4 * tok_rows * route_count // (3 * experts))
    expert_ids = route_ids.reshape(-1)
    onehot = (expert_ids[:, None] == jnp.arange(experts, dtype=jnp.int32)[None, :]).astype(
        jnp.int32
    )
    slot_index = jnp.sum((jnp.cumsum(onehot, axis=0) - onehot) * onehot, axis=1)
    own_residual = lax.dynamic_slice_in_dim(residual_in, col_start, quarter, 1)
    own_stream = (own_residual.astype(jnp.float32) + scatter_sum_mp(partial_value.astype(jnp.bfloat16))).astype(jnp.bfloat16)
    stream = gather_mp(own_stream, 1)
    normed_rows = normalize(stream, norm_gain)
    codes = (expert_ids * capacity + slot_index).reshape(tok_rows, route_count)
    slots = jnp.arange(experts * capacity, dtype=jnp.int32)
    placing = jnp.any(codes[None, :, :] == slots[:, None, None], axis=2).astype(jnp.bfloat16)
    own_normed = lax.dynamic_slice_in_dim(normed_rows, col_start, quarter, 1)
    buffer = jnp.dot(placing, own_normed, preferred_element_type=jnp.float32).astype(jnp.bfloat16)
    buffer = buffer.reshape(experts, capacity, quarter)
    received = lax.all_to_all(buffer, "dp", split_axis=0, concat_axis=0, tiled=True)
    results = run_experts(
        ring_blocks_mp(received.reshape(experts * capacity, quarter)),
        experts,
        capacity,
        w_gate,
        w_up,
        w_down,
    )
    shared_out = shared_experts(normed_rows, shared_gate, shared_up, shared_down, received)
    result_rows = results.reshape(experts * capacity, quarter)
    picked = (
        result_rows[expert_ids * capacity + slot_index]
        .reshape(tok_rows, route_count, quarter)
        .astype(jnp.float32)
    )
    mixture = jnp.einsum("tk,tkc->tc", route_weight, picked, precision=lax.Precision.HIGHEST)
    return (own_stream.astype(jnp.float32) + shared_out.astype(jnp.float32) + mixture).astype(
        jnp.bfloat16
    )


def solution(mesh):
    return jax.shard_map(
        on_device,
        mesh=mesh,
        in_specs=(
            P("dp", "mp"),
            P("dp", None, "mp"),
            P("dp", None, None, "mp"),
            P("dp", None),
            P("dp"),
            P("dp", None, None),
            P("mp", None),
            P("dp", None),
            P(),
            P("dp", None),
            P("dp", None),
            P("dp", None, "mp"),
            P("dp", None, "mp"),
            P("dp", None, "mp"),
            P("dp", "mp"),
            P("dp", "mp"),
            P("mp", "dp"),
        ),
        out_specs=P("dp", "mp"),
        check_vma=False,
    )
```

```python
import jax
import jax.numpy as jnp
from jax import lax
from jax.sharding import PartitionSpec as P

NEGATIVE_FILL = -1e30
EPSILON = 1e-05


def normalize(rows, gain):
    values = rows.astype(jnp.float32)
    mean_square = jnp.mean(values * values, axis=-1, keepdims=True)
    return (values * lax.rsqrt(mean_square + EPSILON) * gain).astype(jnp.bfloat16)


def attend_requests(
    queries, tree_keys, tree_values, tree_allow, kv_cache, page_table, cache_len, score_scale
):
    pool_pages, _, page_rows, head_width = kv_cache.shape
    pool_keys = kv_cache[:, 0].reshape(pool_pages * page_rows, head_width)
    pool_values = kv_cache[:, 1].reshape(pool_pages * page_rows, head_width)
    page_start = jnp.arange(page_table.shape[1], dtype=jnp.int32) * page_rows
    rows_left = cache_len[:, None] - page_start[None, :]
    live_rows = jnp.where(rows_left > 0, jnp.minimum(rows_left, page_rows), 0)
    slot_ids = jnp.arange(pool_pages, dtype=jnp.int32)
    owns = page_table[:, :, None] == slot_ids[None, None, :]
    slot_rows = jnp.sum(jnp.where(owns, live_rows[:, :, None], 0), axis=1)
    row_ids = jnp.arange(page_rows, dtype=jnp.int32)
    live_mask = (row_ids[None, None, :] < slot_rows[:, :, None]).reshape(
        cache_len.shape[0], 1, pool_pages * page_rows
    )
    cache_scores = (
        jnp.einsum("rqd,kd->rqk", queries, pool_keys, preferred_element_type=jnp.float32)
        * score_scale
    )
    cache_scores = jnp.where(live_mask, cache_scores, NEGATIVE_FILL)
    tree_scores = (
        jnp.einsum("rqd,rud->rqu", queries, tree_keys, preferred_element_type=jnp.float32)
        * score_scale
    )
    tree_scores = jnp.where(tree_allow, tree_scores, NEGATIVE_FILL)
    row_peak = jnp.maximum(jnp.max(cache_scores, axis=2), jnp.max(tree_scores, axis=2))[..., None]
    cache_probs = jnp.where(live_mask, jnp.exp(cache_scores - row_peak), 0.0)
    tree_probs = jnp.where(tree_allow, jnp.exp(tree_scores - row_peak), 0.0)
    denom_sum = jnp.sum(cache_probs, axis=2) + jnp.sum(tree_probs, axis=2)
    weighted = jnp.einsum(
        "rqk,kd->rqd", cache_probs.astype(jnp.bfloat16), pool_values,
        preferred_element_type=jnp.float32,
    )
    weighted = weighted + jnp.einsum(
        "rqu,rud->rqd", tree_probs.astype(jnp.bfloat16), tree_values,
        preferred_element_type=jnp.float32,
    )
    return (weighted / denom_sum[..., None]).astype(jnp.bfloat16)


def gather_mp(block, axis):
    parts = lax.axis_size("mp")
    copies = jnp.broadcast_to(block[None], (parts,) + block.shape)
    pieces = lax.all_to_all(copies, "mp", split_axis=0, concat_axis=0, tiled=True)
    pieces = jnp.moveaxis(pieces, 0, axis)
    shape = list(block.shape)
    shape[axis] = shape[axis] * parts
    return pieces.reshape(shape)


def ring_blocks_mp(block):
    parts = lax.axis_size("mp")
    half = block.shape[0] // 2
    to_right = [(k, (k + 1) % parts) for k in range(parts)]
    to_left = [(k, (k - 1) % parts) for k in range(parts)]
    from_left = lax.ppermute(block, "mp", to_right)
    from_right = lax.ppermute(block, "mp", to_left)
    far_top = lax.ppermute(from_right[:half], "mp", to_left)
    far_bottom = lax.ppermute(from_left[half:], "mp", to_right)
    far = jnp.concatenate([far_top, far_bottom], axis=0)
    return [block, from_right, far, from_left]


def blockwise_dot(blocks, weights):
    parts = lax.axis_size("mp")
    mp_index = lax.axis_index("mp")
    width = blocks[0].shape[1]
    total = None
    for step, piece in enumerate(blocks):
        start = ((mp_index + step) % parts) * width
        rows = lax.dynamic_slice_in_dim(weights, start, width, 0)
        term = jnp.dot(piece, rows, preferred_element_type=jnp.float32)
        total = term if total is None else total + term
    return total


def scatter_sum_mp(terms):
    parts = lax.axis_size("mp")
    rows, width = terms.shape
    blocks = terms.reshape(rows, parts, width // parts).transpose(1, 0, 2)
    pieces = lax.all_to_all(blocks, "mp", split_axis=0, concat_axis=0, tiled=True)
    return jnp.sum(pieces.astype(jnp.float32), axis=0)


def run_experts(row_blocks, source_count, slot_count, w_gate, w_up, w_down):
    gate_proj = blockwise_dot(row_blocks, w_gate[0])
    up_proj = blockwise_dot(row_blocks, w_up[0])
    hidden_act = (jax.nn.silu(gate_proj) * up_proj).astype(jnp.bfloat16)
    summed = blockwise_dot(ring_blocks_mp(hidden_act), w_down[0])
    outputs = summed.astype(jnp.bfloat16).reshape(source_count, slot_count, w_down.shape[2])
    return lax.all_to_all(outputs, "dp", split_axis=0, concat_axis=0, tiled=True)


def shared_experts(normed_rows, shared_gate, shared_up, shared_down, after):
    hidden_width = shared_gate.shape[1]
    packed = jnp.concatenate([shared_gate, shared_up, shared_down.T], axis=1)
    packed, after = lax.optimization_barrier((packed, after))
    gathered = lax.all_gather(packed, "dp", axis=0, tiled=True)
    gate_total = jnp.dot(
        normed_rows, gathered[:, :hidden_width], preferred_element_type=jnp.float32
    )
    up_total = jnp.dot(
        normed_rows, gathered[:, hidden_width : 2 * hidden_width], preferred_element_type=jnp.float32
    )
    shared_hidden = (jax.nn.silu(gate_total) * up_total).astype(jnp.bfloat16)
    terms = jnp.einsum(
        "th,dh->td",
        shared_hidden,
        gathered[:, 2 * hidden_width :],
        preferred_element_type=jnp.float32,
    )
    return lax.psum_scatter(terms.astype(jnp.bfloat16), "mp", scatter_dimension=1, tiled=True)


def on_device(
    tree_query,
    new_kv,
    kv_cache,
    page_table,
    cache_len,
    tree_mask,
    out_weight,
    residual_in,
    norm_gain,
    route_ids,
    route_weight,
    w_gate,
    w_up,
    w_down,
    shared_gate,
    shared_up,
    shared_down,
):
    tok_rows = tree_query.shape[0]
    req_count = cache_len.shape[0]
    tree_len = tree_mask.shape[1]
    head_width = new_kv.shape[2]
    local_heads = tree_query.shape[1] // head_width
    score_scale = head_width ** (-0.5)
    queries = tree_query.reshape(req_count, tree_len, local_heads, head_width)
    queries = queries.transpose(0, 2, 1, 3).reshape(req_count, local_heads * tree_len, head_width)
    tree_keys = new_kv[:, 0, :].reshape(req_count, tree_len, head_width)
    tree_values = new_kv[:, 1, :].reshape(req_count, tree_len, head_width)
    tree_allow = jnp.tile(tree_mask, (1, local_heads, 1)) == 1
    attended = attend_requests(
        queries, tree_keys, tree_values, tree_allow, kv_cache, page_table, cache_len, score_scale
    )
    attended = attended.reshape(req_count, local_heads, tree_len, head_width).transpose(0, 2, 1, 3)
    attended = attended.reshape(tok_rows, local_heads * head_width)
    partial_value = jnp.dot(attended, out_weight, preferred_element_type=jnp.float32)
    model_width = residual_in.shape[1]
    quarter = model_width // lax.axis_size("mp")
    col_start = lax.axis_index("mp") * quarter
    experts = lax.axis_size("dp") * w_gate.shape[0]
    route_count = route_ids.shape[1]
    capacity = min(tok_rows, 4 * tok_rows * route_count // (3 * experts))
    expert_ids = route_ids.reshape(-1)
    onehot = (expert_ids[:, None] == jnp.arange(experts, dtype=jnp.int32)[None, :]).astype(
        jnp.int32
    )
    slot_index = jnp.sum((jnp.cumsum(onehot, axis=0) - onehot) * onehot, axis=1)
    own_residual = lax.dynamic_slice_in_dim(residual_in, col_start, quarter, 1)
    own_stream = (own_residual.astype(jnp.float32) + scatter_sum_mp(partial_value)).astype(jnp.bfloat16)
    stream = jnp.roll(
        jnp.concatenate(ring_blocks_mp(own_stream), axis=1), lax.axis_index("mp") * quarter, axis=1
    )
    normed_rows = normalize(stream, norm_gain)
    codes = (expert_ids * capacity + slot_index).reshape(tok_rows, route_count)
    slots = jnp.arange(experts * capacity, dtype=jnp.int32)
    placing = jnp.any(codes[None, :, :] == slots[:, None, None], axis=2).astype(jnp.bfloat16)
    own_normed = lax.dynamic_slice_in_dim(normed_rows, col_start, quarter, 1)
    buffer = jnp.dot(placing, own_normed, preferred_element_type=jnp.float32).astype(jnp.bfloat16)
    buffer = buffer.reshape(experts, capacity, quarter)
    received = lax.all_to_all(buffer, "dp", split_axis=0, concat_axis=0, tiled=True)
    results = run_experts(
        ring_blocks_mp(received.reshape(experts * capacity, quarter)),
        experts,
        capacity,
        w_gate,
        w_up,
        w_down,
    )
    shared_out = shared_experts(normed_rows, shared_gate, shared_up, shared_down, received)
    result_rows = results.reshape(experts * capacity, quarter)
    picked = (
        result_rows[expert_ids * capacity + slot_index]
        .reshape(tok_rows, route_count, quarter)
        .astype(jnp.float32)
    )
    mixture = jnp.einsum("tk,tkc->tc", route_weight, picked, precision=lax.Precision.HIGHEST)
    return (own_stream.astype(jnp.float32) + shared_out.astype(jnp.float32) + mixture).astype(
        jnp.bfloat16
    )


def solution(mesh):
    return jax.shard_map(
        on_device,
        mesh=mesh,
        in_specs=(
            P("dp", "mp"),
            P("dp", None, "mp"),
            P("dp", None, None, "mp"),
            P("dp", None),
            P("dp"),
            P("dp", None, None),
            P("mp", None),
            P("dp", None),
            P(),
            P("dp", None),
            P("dp", None),
            P("dp", None, "mp"),
            P("dp", None, "mp"),
            P("dp", None, "mp"),
            P("dp", "mp"),
            P("dp", "mp"),
            P("mp", "dp"),
        ),
        out_specs=P("dp", "mp"),
        check_vma=False,
    )
```

```python
import jax
import jax.numpy as jnp
from jax import lax
from jax.sharding import PartitionSpec as P

NEGATIVE_FILL = -1e30
EPSILON = 1e-05


def normalize(rows, gain):
    values = rows.astype(jnp.float32)
    mean_square = jnp.mean(values * values, axis=-1, keepdims=True)
    return (values * lax.rsqrt(mean_square + EPSILON) * gain).astype(jnp.bfloat16)


def attend_requests(
    queries, tree_keys, tree_values, tree_allow, kv_cache, page_table, cache_len, score_scale
):
    pool_pages, _, page_rows, head_width = kv_cache.shape
    pool_keys = kv_cache[:, 0].reshape(pool_pages * page_rows, head_width)
    pool_values = kv_cache[:, 1].reshape(pool_pages * page_rows, head_width)
    page_start = jnp.arange(page_table.shape[1], dtype=jnp.int32) * page_rows
    rows_left = cache_len[:, None] - page_start[None, :]
    live_rows = jnp.where(rows_left > 0, jnp.minimum(rows_left, page_rows), 0)
    slot_ids = jnp.arange(pool_pages, dtype=jnp.int32)
    owns = page_table[:, :, None] == slot_ids[None, None, :]
    slot_rows = jnp.sum(jnp.where(owns, live_rows[:, :, None], 0), axis=1)
    row_ids = jnp.arange(page_rows, dtype=jnp.int32)
    live_mask = (row_ids[None, None, :] < slot_rows[:, :, None]).reshape(
        cache_len.shape[0], 1, pool_pages * page_rows
    )
    cache_scores = (
        jnp.einsum("rqd,kd->rqk", queries, pool_keys, preferred_element_type=jnp.float32)
        * score_scale
    )
    cache_scores = jnp.where(live_mask, cache_scores, NEGATIVE_FILL)
    tree_scores = (
        jnp.einsum("rqd,rud->rqu", queries, tree_keys, preferred_element_type=jnp.float32)
        * score_scale
    )
    tree_scores = jnp.where(tree_allow, tree_scores, NEGATIVE_FILL)
    row_peak = jnp.maximum(jnp.max(cache_scores, axis=2), jnp.max(tree_scores, axis=2))[..., None]
    cache_probs = jnp.where(live_mask, jnp.exp(cache_scores - row_peak), 0.0)
    tree_probs = jnp.where(tree_allow, jnp.exp(tree_scores - row_peak), 0.0)
    denom_sum = jnp.sum(cache_probs, axis=2) + jnp.sum(tree_probs, axis=2)
    weighted = jnp.einsum(
        "rqk,kd->rqd", cache_probs.astype(jnp.bfloat16), pool_values,
        preferred_element_type=jnp.float32,
    )
    weighted = weighted + jnp.einsum(
        "rqu,rud->rqd", tree_probs.astype(jnp.bfloat16), tree_values,
        preferred_element_type=jnp.float32,
    )
    return (weighted / denom_sum[..., None]).astype(jnp.bfloat16)


def gather_mp(block, axis):
    parts = lax.axis_size("mp")
    copies = jnp.broadcast_to(block[None], (parts,) + block.shape)
    pieces = lax.all_to_all(copies, "mp", split_axis=0, concat_axis=0, tiled=True)
    pieces = jnp.moveaxis(pieces, 0, axis)
    shape = list(block.shape)
    shape[axis] = shape[axis] * parts
    return pieces.reshape(shape)


def ring_blocks_mp(block):
    parts = lax.axis_size("mp")
    half = block.shape[0] // 2
    to_right = [(k, (k + 1) % parts) for k in range(parts)]
    to_left = [(k, (k - 1) % parts) for k in range(parts)]
    from_left = lax.ppermute(block, "mp", to_right)
    from_right = lax.ppermute(block, "mp", to_left)
    far_top = lax.ppermute(from_right[:half], "mp", to_left)
    far_bottom = lax.ppermute(from_left[half:], "mp", to_right)
    far = jnp.concatenate([far_top, far_bottom], axis=0)
    return [block, from_right, far, from_left]


def blockwise_dot(blocks, weights):
    parts = lax.axis_size("mp")
    mp_index = lax.axis_index("mp")
    width = blocks[0].shape[1]
    total = None
    for step, piece in enumerate(blocks):
        start = ((mp_index + step) % parts) * width
        rows = lax.dynamic_slice_in_dim(weights, start, width, 0)
        term = jnp.dot(piece, rows, preferred_element_type=jnp.float32)
        total = term if total is None else total + term
    return total


def scatter_sum_mp(terms):
    parts = lax.axis_size("mp")
    rows, width = terms.shape
    blocks = terms.reshape(rows, parts, width // parts).transpose(1, 0, 2)
    pieces = lax.all_to_all(blocks, "mp", split_axis=0, concat_axis=0, tiled=True)
    return jnp.sum(pieces.astype(jnp.float32), axis=0)


def run_experts(row_blocks, source_count, slot_count, w_gate, w_up, w_down):
    gate_proj = blockwise_dot(row_blocks, w_gate[0])
    up_proj = blockwise_dot(row_blocks, w_up[0])
    hidden_act = (jax.nn.silu(gate_proj) * up_proj).astype(jnp.bfloat16)
    summed = blockwise_dot(ring_blocks_mp(hidden_act), w_down[0])
    outputs = summed.astype(jnp.bfloat16).reshape(source_count, slot_count, w_down.shape[2])
    return lax.all_to_all(outputs, "dp", split_axis=0, concat_axis=0, tiled=True)


def shared_experts(normed_rows, shared_gate, shared_up, shared_down, after):
    hidden_width = shared_gate.shape[1]
    packed = jnp.concatenate([shared_gate, shared_up, shared_down.T], axis=1)
    packed, after = lax.optimization_barrier((packed, after))
    gathered = lax.all_gather(packed, "dp", axis=0, tiled=True)
    gate_total = jnp.dot(
        normed_rows, gathered[:, :hidden_width], preferred_element_type=jnp.float32
    )
    up_total = jnp.dot(
        normed_rows, gathered[:, hidden_width : 2 * hidden_width], preferred_element_type=jnp.float32
    )
    shared_hidden = (jax.nn.silu(gate_total) * up_total).astype(jnp.bfloat16)
    terms = jnp.einsum(
        "th,dh->td",
        shared_hidden,
        gathered[:, 2 * hidden_width :],
        preferred_element_type=jnp.float32,
    )
    return lax.psum_scatter(terms.astype(jnp.bfloat16), "mp", scatter_dimension=1, tiled=True)


def on_device(
    tree_query,
    new_kv,
    kv_cache,
    page_table,
    cache_len,
    tree_mask,
    out_weight,
    residual_in,
    norm_gain,
    route_ids,
    route_weight,
    w_gate,
    w_up,
    w_down,
    shared_gate,
    shared_up,
    shared_down,
):
    tok_rows = tree_query.shape[0]
    req_count = cache_len.shape[0]
    tree_len = tree_mask.shape[1]
    head_width = new_kv.shape[2]
    local_heads = tree_query.shape[1] // head_width
    score_scale = head_width ** (-0.5)
    queries = tree_query.reshape(req_count, tree_len, local_heads, head_width)
    queries = queries.transpose(0, 2, 1, 3).reshape(req_count, local_heads * tree_len, head_width)
    tree_keys = new_kv[:, 0, :].reshape(req_count, tree_len, head_width)
    tree_values = new_kv[:, 1, :].reshape(req_count, tree_len, head_width)
    tree_allow = jnp.tile(tree_mask, (1, local_heads, 1)) == 1
    attended = attend_requests(
        queries, tree_keys, tree_values, tree_allow, kv_cache, page_table, cache_len, score_scale
    )
    attended = attended.reshape(req_count, local_heads, tree_len, head_width).transpose(0, 2, 1, 3)
    attended = attended.reshape(tok_rows, local_heads * head_width)
    partial_value = jnp.dot(attended, out_weight, preferred_element_type=jnp.float32)
    model_width = residual_in.shape[1]
    quarter = model_width // lax.axis_size("mp")
    col_start = lax.axis_index("mp") * quarter
    experts = lax.axis_size("dp") * w_gate.shape[0]
    route_count = route_ids.shape[1]
    capacity = min(tok_rows, 4 * tok_rows * route_count // (3 * experts))
    expert_ids = route_ids.reshape(-1)
    onehot = (expert_ids[:, None] == jnp.arange(experts, dtype=jnp.int32)[None, :]).astype(
        jnp.int32
    )
    slot_index = jnp.sum((jnp.cumsum(onehot, axis=0) - onehot) * onehot, axis=1)
    own_residual = lax.dynamic_slice_in_dim(residual_in, col_start, quarter, 1)
    own_stream = (own_residual.astype(jnp.float32) + scatter_sum_mp(partial_value)).astype(jnp.bfloat16)
    stream = gather_mp(own_stream, 1)
    normed_rows = normalize(stream, norm_gain)
    codes = (expert_ids * capacity + slot_index).reshape(tok_rows, route_count)
    slots = jnp.arange(experts * capacity, dtype=jnp.int32)
    placing = jnp.any(codes[None, :, :] == slots[:, None, None], axis=2).astype(jnp.bfloat16)
    own_normed = lax.dynamic_slice_in_dim(normed_rows, col_start, quarter, 1)
    buffer = jnp.dot(placing, own_normed, preferred_element_type=jnp.float32).astype(jnp.bfloat16)
    buffer = buffer.reshape(experts, capacity, quarter)
    received = lax.all_to_all(buffer, "dp", split_axis=0, concat_axis=0, tiled=True)
    results = run_experts(
        ring_blocks_mp(received.reshape(experts * capacity, quarter)),
        experts,
        capacity,
        w_gate,
        w_up,
        w_down,
    )
    shared_out = shared_experts(normed_rows, shared_gate, shared_up, shared_down, received)
    result_rows = results.reshape(experts * capacity, quarter)
    mixing = jnp.sum(
        jnp.where(codes[:, :, None] == slots[None, None, :], route_weight[:, :, None], 0.0), axis=1
    )
    mixture = jnp.dot(
        mixing, result_rows.astype(jnp.float32), precision=lax.Precision.HIGHEST,
        preferred_element_type=jnp.float32,
    )
    return (own_stream.astype(jnp.float32) + shared_out.astype(jnp.float32) + mixture).astype(
        jnp.bfloat16
    )


def solution(mesh):
    return jax.shard_map(
        on_device,
        mesh=mesh,
        in_specs=(
            P("dp", "mp"),
            P("dp", None, "mp"),
            P("dp", None, None, "mp"),
            P("dp", None),
            P("dp"),
            P("dp", None, None),
            P("mp", None),
            P("dp", None),
            P(),
            P("dp", None),
            P("dp", None),
            P("dp", None, "mp"),
            P("dp", None, "mp"),
            P("dp", None, "mp"),
            P("dp", "mp"),
            P("dp", "mp"),
            P("mp", "dp"),
        ),
        out_specs=P("dp", "mp"),
        check_vma=False,
    )
```

```python
import jax
import jax.numpy as jnp
from jax import lax
from jax.sharding import PartitionSpec as P

NEGATIVE_FILL = -1e30
EPSILON = 1e-05


def normalize(rows, gain):
    values = rows.astype(jnp.float32)
    mean_square = jnp.mean(values * values, axis=-1, keepdims=True)
    return (values * lax.rsqrt(mean_square + EPSILON) * gain).astype(jnp.bfloat16)


def attend_requests(
    queries, tree_keys, tree_values, tree_allow, kv_cache, page_table, cache_len, score_scale
):
    pool_pages, _, page_rows, head_width = kv_cache.shape
    pool_keys = kv_cache[:, 0].reshape(pool_pages * page_rows, head_width)
    pool_values = kv_cache[:, 1].reshape(pool_pages * page_rows, head_width)
    page_start = jnp.arange(page_table.shape[1], dtype=jnp.int32) * page_rows
    rows_left = cache_len[:, None] - page_start[None, :]
    live_rows = jnp.where(rows_left > 0, jnp.minimum(rows_left, page_rows), 0)
    slot_ids = jnp.arange(pool_pages, dtype=jnp.int32)
    owns = page_table[:, :, None] == slot_ids[None, None, :]
    slot_rows = jnp.sum(jnp.where(owns, live_rows[:, :, None], 0), axis=1)
    row_ids = jnp.arange(page_rows, dtype=jnp.int32)
    live_mask = (row_ids[None, None, :] < slot_rows[:, :, None]).reshape(
        cache_len.shape[0], 1, pool_pages * page_rows
    )
    cache_scores = (
        jnp.einsum("rqd,kd->rqk", queries, pool_keys, preferred_element_type=jnp.float32)
        * score_scale
    )
    cache_scores = jnp.where(live_mask, cache_scores, NEGATIVE_FILL)
    tree_scores = (
        jnp.einsum("rqd,rud->rqu", queries, tree_keys, preferred_element_type=jnp.float32)
        * score_scale
    )
    tree_scores = jnp.where(tree_allow, tree_scores, NEGATIVE_FILL)
    row_peak = jnp.maximum(jnp.max(cache_scores, axis=2), jnp.max(tree_scores, axis=2))[..., None]
    cache_probs = jnp.where(live_mask, jnp.exp(cache_scores - row_peak), 0.0)
    tree_probs = jnp.where(tree_allow, jnp.exp(tree_scores - row_peak), 0.0)
    denom_sum = jnp.sum(cache_probs, axis=2) + jnp.sum(tree_probs, axis=2)
    weighted = jnp.einsum(
        "rqk,kd->rqd", cache_probs.astype(jnp.bfloat16), pool_values,
        preferred_element_type=jnp.float32,
    )
    weighted = weighted + jnp.einsum(
        "rqu,rud->rqd", tree_probs.astype(jnp.bfloat16), tree_values,
        preferred_element_type=jnp.float32,
    )
    return (weighted / denom_sum[..., None]).astype(jnp.bfloat16)


def gather_mp(block, axis):
    parts = lax.axis_size("mp")
    copies = jnp.broadcast_to(block[None], (parts,) + block.shape)
    pieces = lax.all_to_all(copies, "mp", split_axis=0, concat_axis=0, tiled=True)
    pieces = jnp.moveaxis(pieces, 0, axis)
    shape = list(block.shape)
    shape[axis] = shape[axis] * parts
    return pieces.reshape(shape)


def ring_blocks_mp(block):
    parts = lax.axis_size("mp")
    half = block.shape[0] // 2
    to_right = [(k, (k + 1) % parts) for k in range(parts)]
    to_left = [(k, (k - 1) % parts) for k in range(parts)]
    from_left = lax.ppermute(block, "mp", to_right)
    from_right = lax.ppermute(block, "mp", to_left)
    far_top = lax.ppermute(from_right[:half], "mp", to_left)
    far_bottom = lax.ppermute(from_left[half:], "mp", to_right)
    return [
        (block[:half], block[half:]),
        (from_right[:half], from_right[half:]),
        (far_top, far_bottom),
        (from_left[:half], from_left[half:]),
    ]


def blockwise_dot(blocks, weights):
    parts = lax.axis_size("mp")
    mp_index = lax.axis_index("mp")
    width = blocks[0][0].shape[1]
    totals = [None, None]
    for step, halves in enumerate(blocks):
        start = ((mp_index + step) % parts) * width
        rows = lax.dynamic_slice_in_dim(weights, start, width, 0)
        for side, piece in enumerate(halves):
            term = jnp.dot(piece, rows, preferred_element_type=jnp.float32)
            totals[side] = term if totals[side] is None else totals[side] + term
    return jnp.concatenate(totals, axis=0)


def scatter_sum_mp(terms):
    parts = lax.axis_size("mp")
    rows, width = terms.shape
    blocks = terms.reshape(rows, parts, width // parts).transpose(1, 0, 2)
    pieces = lax.all_to_all(blocks, "mp", split_axis=0, concat_axis=0, tiled=True)
    return jnp.sum(pieces.astype(jnp.float32), axis=0)


def run_experts(row_blocks, source_count, slot_count, w_gate, w_up, w_down):
    gate_proj = blockwise_dot(row_blocks, w_gate[0])
    up_proj = blockwise_dot(row_blocks, w_up[0])
    hidden_act = (jax.nn.silu(gate_proj) * up_proj).astype(jnp.bfloat16)
    summed = blockwise_dot(ring_blocks_mp(hidden_act), w_down[0])
    outputs = summed.astype(jnp.bfloat16).reshape(source_count, slot_count, w_down.shape[2])
    return lax.all_to_all(outputs, "dp", split_axis=0, concat_axis=0, tiled=True)


def shared_experts(normed_rows, shared_gate, shared_up, shared_down, after):
    hidden_width = shared_gate.shape[1]
    packed = jnp.concatenate([shared_gate, shared_up, shared_down.T], axis=1)
    packed, after = lax.optimization_barrier((packed, after))
    gathered = lax.all_gather(packed, "dp", axis=0, tiled=True)
    gate_total = jnp.dot(
        normed_rows, gathered[:, :hidden_width], preferred_element_type=jnp.float32
    )
    up_total = jnp.dot(
        normed_rows, gathered[:, hidden_width : 2 * hidden_width], preferred_element_type=jnp.float32
    )
    shared_hidden = (jax.nn.silu(gate_total) * up_total).astype(jnp.bfloat16)
    terms = jnp.einsum(
        "th,dh->td",
        shared_hidden,
        gathered[:, 2 * hidden_width :],
        preferred_element_type=jnp.float32,
    )
    return lax.psum_scatter(terms.astype(jnp.bfloat16), "mp", scatter_dimension=1, tiled=True)


def on_device(
    tree_query,
    new_kv,
    kv_cache,
    page_table,
    cache_len,
    tree_mask,
    out_weight,
    residual_in,
    norm_gain,
    route_ids,
    route_weight,
    w_gate,
    w_up,
    w_down,
    shared_gate,
    shared_up,
    shared_down,
):
    tok_rows = tree_query.shape[0]
    req_count = cache_len.shape[0]
    tree_len = tree_mask.shape[1]
    head_width = new_kv.shape[2]
    local_heads = tree_query.shape[1] // head_width
    score_scale = head_width ** (-0.5)
    queries = tree_query.reshape(req_count, tree_len, local_heads, head_width)
    queries = queries.transpose(0, 2, 1, 3).reshape(req_count, local_heads * tree_len, head_width)
    tree_keys = new_kv[:, 0, :].reshape(req_count, tree_len, head_width)
    tree_values = new_kv[:, 1, :].reshape(req_count, tree_len, head_width)
    tree_allow = jnp.tile(tree_mask, (1, local_heads, 1)) == 1
    attended = attend_requests(
        queries, tree_keys, tree_values, tree_allow, kv_cache, page_table, cache_len, score_scale
    )
    attended = attended.reshape(req_count, local_heads, tree_len, head_width).transpose(0, 2, 1, 3)
    attended = attended.reshape(tok_rows, local_heads * head_width)
    partial_value = jnp.dot(attended, out_weight, preferred_element_type=jnp.float32)
    model_width = residual_in.shape[1]
    quarter = model_width // lax.axis_size("mp")
    col_start = lax.axis_index("mp") * quarter
    experts = lax.axis_size("dp") * w_gate.shape[0]
    route_count = route_ids.shape[1]
    capacity = min(tok_rows, 4 * tok_rows * route_count // (3 * experts))
    expert_ids = route_ids.reshape(-1)
    onehot = (expert_ids[:, None] == jnp.arange(experts, dtype=jnp.int32)[None, :]).astype(
        jnp.int32
    )
    slot_index = jnp.sum((jnp.cumsum(onehot, axis=0) - onehot) * onehot, axis=1)
    own_residual = lax.dynamic_slice_in_dim(residual_in, col_start, quarter, 1)
    own_stream = (own_residual.astype(jnp.float32) + scatter_sum_mp(partial_value)).astype(jnp.bfloat16)
    stream = gather_mp(own_stream, 1)
    normed_rows = normalize(stream, norm_gain)
    codes = (expert_ids * capacity + slot_index).reshape(tok_rows, route_count)
    slots = jnp.arange(experts * capacity, dtype=jnp.int32)
    placing = jnp.any(codes[None, :, :] == slots[:, None, None], axis=2).astype(jnp.bfloat16)
    own_normed = lax.dynamic_slice_in_dim(normed_rows, col_start, quarter, 1)
    buffer = jnp.dot(placing, own_normed, preferred_element_type=jnp.float32).astype(jnp.bfloat16)
    buffer = buffer.reshape(experts, capacity, quarter)
    received = lax.all_to_all(buffer, "dp", split_axis=0, concat_axis=0, tiled=True)
    results = run_experts(
        ring_blocks_mp(received.reshape(experts * capacity, quarter)),
        experts,
        capacity,
        w_gate,
        w_up,
        w_down,
    )
    shared_out = shared_experts(normed_rows, shared_gate, shared_up, shared_down, received)
    result_rows = results.reshape(experts * capacity, quarter)
    picked = (
        result_rows[expert_ids * capacity + slot_index]
        .reshape(tok_rows, route_count, quarter)
        .astype(jnp.float32)
    )
    mixture = jnp.einsum("tk,tkc->tc", route_weight, picked, precision=lax.Precision.HIGHEST)
    return (own_stream.astype(jnp.float32) + shared_out.astype(jnp.float32) + mixture).astype(
        jnp.bfloat16
    )


def solution(mesh):
    return jax.shard_map(
        on_device,
        mesh=mesh,
        in_specs=(
            P("dp", "mp"),
            P("dp", None, "mp"),
            P("dp", None, None, "mp"),
            P("dp", None),
            P("dp"),
            P("dp", None, None),
            P("mp", None),
            P("dp", None),
            P(),
            P("dp", None),
            P("dp", None),
            P("dp", None, "mp"),
            P("dp", None, "mp"),
            P("dp", None, "mp"),
            P("dp", "mp"),
            P("dp", "mp"),
            P("mp", "dp"),
        ),
        out_specs=P("dp", "mp"),
        check_vma=False,
    )
```
